32 devices in a mesh: req: 4 (over x, core), tok: 8 (over z, y).
Axes of the slice: x: 2, y: 2, z: 4, core: 2. Of those that a mesh axis runs over, the one named last changes fastest.
Arguments:
- queries: bfloat16 [8, 2048, 2048], P('req', 'tok'), may hold values from -16 to 16
- new_kv: bfloat16 [8, 2048, 256], P('req', 'tok'), may hold values from -6 to 6
- cache_kv: bfloat16 [8, 4096, 256], P('req', 'tok'), may hold values from -6 to 6
- residual: bfloat16 [8, 2048, 2048], P('req', 'tok'), may hold values from -24 to 24
- prefix_len: int32 [8], replicated, may hold values from 0 to 4096, as said below
- dest_map: int32 [8, 2048], P('req', 'tok'), may hold values from -1 to 4095, as said below
- w_out: bfloat16 [2048, 2048], replicated, may hold values from -0.125 to 0.125
- b_out: float32 [2048], replicated, may hold values from -4 to 4
- ln_gain: float32 [2048], replicated, may hold values from 0.1 to 1.9
- ln_bias: float32 [2048], replicated, may hold values from -4 to 4
- w_up: bfloat16 [2048, 8192], P(None, 'tok'), may hold values from -0.125 to 0.125
- b_up: float32 [8192], P('tok'), may hold values from -6 to 6
- w_down: bfloat16 [8192, 2048], P('tok'), may hold values from -0.0625 to 0.0625
- b_down: float32 [2048], replicated, may hold values from -4 to 4
Outputs:
- layer_out: bfloat16 [4096, 2048], P(('req', 'tok'))
The draws below stay inside these ranges and needn't reach their ends.
Inputs may be any that keep to these rules, and one draw needn't show every extreme that they name: `prefix_len`: some request uses all 4096 cached positions. In each request the slots that are not -1 are its first n, with n from 128 to 2048; the n over all requests sum to 4096 and the largest is exactly 2048. These slots hold distinct rows of layer_out, every row held by exactly one of them. The live slots of one device's block of dest_map name at most 16 rows of any one device's block of layer_out.
All inputs are finite; a program needn't handle non-finite values.
Results may differ from the reference program's by a relative error of at most 0.012.
Values may be sent and summed in bfloat16 or wider, within the bound.
No kernel may reach another device: no remote copies, remote signals or barrier semaphores. Data moves between devices by JAX's collectives and lax.ppermute only.
A program may use at most 192 MiB of HBM per device.

```python
import math
import jax
import jax.numpy as jnp
from jax import lax

D = 2048
HEADS = 16
HEAD_DIM = 128
FF = 8192
SLOTS = 2048
PREFIX = 4096
LEN_MIN = 128
REQ_DEV = 2
TOK_DEV = 128
REQS = 8
SLOT_DEV = 256
TOKENS = 4096
N_REQ = 4
N_TOK = 8


def layout_draw(key):
    own_key = jax.random.fold_in(key, 404)
    pick_key, weight_key, prefix_key, deep_key, shuffle_key = jax.random.split(own_key, 5)
    room = SLOTS - LEN_MIN
    spare = TOKENS - REQS * LEN_MIN - room
    req_order = jnp.arange(REQS, dtype=jnp.int32)
    longest = jax.random.randint(pick_key, (), 0, REQS)
    weights = jnp.where(req_order == longest, 0, jax.random.randint(weight_key, (REQS,), 1, 1000))
    shares = jnp.minimum(spare * weights // jnp.sum(weights), room)
    spaces = jnp.where(req_order == longest, 0, room - shares)
    before = jnp.cumsum(spaces) - spaces
    leftover = spare - jnp.sum(shares)
    extras = shares + jnp.clip(leftover - before, 0, spaces)
    extras = jnp.where(req_order == longest, room, extras)
    lengths = (LEN_MIN + extras).astype(jnp.int32)
    prefixes = jax.random.randint(prefix_key, (REQS,), 0, PREFIX + 1)
    deepest = jax.random.randint(deep_key, (), 0, REQS)
    prefixes = jnp.where(req_order == deepest, PREFIX, prefixes).astype(jnp.int32)
    slot_index = jnp.arange(SLOTS, dtype=jnp.int32)[None, :]
    is_live = (slot_index < lengths[:, None]).astype(jnp.int32)
    ordered = is_live.reshape(N_REQ, REQ_DEV, N_TOK, SLOT_DEV).transpose(0, 2, 1, 3).reshape(-1)
    ranked = jnp.cumsum(ordered) - 1
    ranked = ranked.reshape(N_REQ, N_TOK, REQ_DEV, SLOT_DEV).transpose(0, 2, 1, 3).reshape(REQS, SLOTS)
    ranked = jnp.maximum(ranked, 0)
    all_devices = N_REQ * N_TOK
    shuffled = jax.random.permutation(shuffle_key, all_devices)
    target = shuffled[ranked % all_devices] * TOK_DEV + ranked // all_devices
    target = jnp.where(is_live > 0, target, -1).astype(jnp.int32)
    return (prefixes, target)


def draw_prefix_len(key, part):
    return layout_draw(key)[0]


def draw_dest_map(key, part):
    return layout_draw(key)[1]


def draw_queries(key, part):
    own_key = jax.random.fold_in(key, 101)
    values = jnp.clip(2.5 * jax.random.normal(own_key, (REQS, SLOTS, HEADS, HEAD_DIM), jnp.float32), -16.0, 16.0)
    return values.reshape(REQS, SLOTS, HEADS * HEAD_DIM).astype(jnp.bfloat16)


def draw_new_kv(key, part):
    own_key = jax.random.fold_in(key, 202)
    values = jnp.clip(jax.random.normal(own_key, (REQS, SLOTS, 2 * HEAD_DIM), jnp.float32), -6.0, 6.0)
    return values.astype(jnp.bfloat16)


def draw_residual(key, part):
    own_key = jax.random.fold_in(key, 303)
    first_key = jax.random.fold_in(own_key, 0)
    third_key = jax.random.fold_in(own_key, 2)
    columns = jnp.exp(jax.random.uniform(first_key, (HEADS * HEAD_DIM,), jnp.float32, math.log(0.3), math.log(3.0)))
    values = jnp.clip(jax.random.normal(third_key, (REQS, SLOTS, HEADS * HEAD_DIM), jnp.float32), -6.0, 6.0)
    return jnp.clip(values * columns, -24.0, 24.0).astype(jnp.bfloat16)


def block_scale(rng, extent, pieces, smallest, largest):
    loudness, own = 1.0, jax.random.fold_in(rng, 6)
    for position, blocks in pieces:
        steps = jnp.exp(jax.random.uniform(jax.random.fold_in(own, position), (blocks,), jnp.float32, smallest / len(pieces), largest / len(pieces)))
        loudness = loudness * jnp.repeat(steps, extent[position] // blocks).reshape([-1 if axis == position else 1 for axis in range(len(extent))])
    return loudness


def bell_draw(key, shape, spread, most, pieces=(), held_as=jnp.bfloat16):
    drawn = spread * jax.random.normal(key, shape, jnp.float32)
    if pieces:
        drawn = drawn * block_scale(key, shape, pieces, -0.22, 0.18)
    return jnp.clip(drawn, -most, most).astype(held_as)


def setup_inputs(seed: int = 0) -> dict:
    key_list = jax.random.split(jax.random.key(seed), 15)
    queries = draw_queries(jax.random.fold_in(key_list[14], 71), 0)
    new_kv = draw_new_kv(jax.random.fold_in(key_list[14], 71), 0)
    cache_kv = bell_draw(key_list[2], (REQS, PREFIX, 2 * HEAD_DIM), 1.0, 6.0, ((0, 4), (1, 8)))
    residual = draw_residual(jax.random.fold_in(key_list[14], 71), 0)
    prefix_len = draw_prefix_len(jax.random.fold_in(key_list[14], 71), 0)
    dest_map = draw_dest_map(jax.random.fold_in(key_list[14], 71), 0)
    w_out = bell_draw(key_list[6], (D, D), D ** -0.5, 0.125)
    b_out = bell_draw(key_list[7], (D,), 0.3, 4.0, (), jnp.float32)
    ln_gain = jnp.clip(1.0 + 0.18 * jax.random.normal(key_list[8], (D,), jnp.float32), 0.1, 1.9)
    ln_bias = bell_draw(key_list[9], (D,), 0.3, 4.0, (), jnp.float32)
    w_up = bell_draw(key_list[10], (D, FF), D ** -0.5, 0.125, ((1, 8),))
    b_up = bell_draw(key_list[11], (FF,), 0.5, 6.0, ((0, 8),), jnp.float32)
    w_down = bell_draw(key_list[12], (FF, D), FF ** -0.5, 0.0625, ((0, 8),))
    b_down = bell_draw(key_list[13], (D,), 0.3, 4.0, (), jnp.float32)
    return {"queries": queries, "new_kv": new_kv, "cache_kv": cache_kv, "residual": residual, "prefix_len": prefix_len, "dest_map": dest_map, "w_out": w_out, "b_out": b_out, "ln_gain": ln_gain, "ln_bias": ln_bias, "w_up": w_up, "b_up": b_up, "w_down": w_down, "b_down": b_down}


neg_large = -1e+30
ln_eps = 1e-05

def settle(values):
    return lax.optimization_barrier(values.astype(jnp.bfloat16)).astype(jnp.float32)

def one_request(item, w_out, b_out, ln_gain, ln_bias, w_up, b_up, down_blocks, b_down):
    queries, new_kv, cache_kv, residual, prefix = item
    width = HEADS * HEAD_DIM
    stacked = jnp.concatenate([cache_kv, new_kv], axis=0).astype(jnp.float32)
    key_part = stacked[:, :HEAD_DIM]
    value_part = stacked[:, HEAD_DIM:]
    cache_pos = jnp.arange(PREFIX, dtype=jnp.int32)
    new_pos = jnp.arange(SLOTS, dtype=jnp.int32)
    rows_block = min(512, SLOTS)
    blocks = SLOTS // rows_block
    query_blocks = queries.reshape(blocks, rows_block, HEADS, HEAD_DIM)
    residual_blocks = residual.reshape(blocks, rows_block, width)
    starts = jnp.arange(blocks, dtype=jnp.int32) * rows_block
    scale = 1.0 / math.sqrt(HEAD_DIM)

    def block_rows(section):
        query_part, residual_part, start = section
        query_pos = start + jnp.arange(rows_block, dtype=jnp.int32)
        cache_seen = jnp.broadcast_to(cache_pos[None, :] < prefix, (rows_block, PREFIX))
        new_seen = new_pos[None, :] <= query_pos[:, None]
        visible = jnp.concatenate([cache_seen, new_seen], axis=1)
        scores = jnp.einsum('qhd,kd->hqk', query_part.astype(jnp.float32), key_part) * scale
        scores = jnp.where(visible[None], scores, neg_large)
        weights = settle(jax.nn.softmax(scores, axis=-1))
        attended = jnp.einsum('hqk,kd->qhd', weights, value_part).reshape(rows_block, width)
        attended = attended.astype(jnp.bfloat16)
        hidden_f = residual_part.astype(jnp.float32) + jnp.dot(attended, w_out, preferred_element_type=jnp.float32) + b_out
        hidden_state = hidden_f.astype(jnp.bfloat16)
        state_f = hidden_state.astype(jnp.float32)
        mean = lax.optimization_barrier(jnp.mean(state_f, axis=-1, keepdims=True))
        centered = state_f - mean
        variance = lax.optimization_barrier(jnp.mean(centered * centered, axis=-1, keepdims=True))
        normed = (centered * lax.rsqrt(variance + ln_eps) * ln_gain + ln_bias).astype(jnp.bfloat16)
        units = jax.nn.gelu(jnp.dot(normed, w_up, preferred_element_type=jnp.float32) + b_up, approximate=True)
        units = units.astype(jnp.bfloat16).astype(jnp.float32)
        units = units.reshape(rows_block, N_TOK, FF // N_TOK)
        partial_value = jnp.einsum('qkf,kfd->kqd', units, down_blocks)
        summed = lax.optimization_barrier(jnp.sum(settle(partial_value), axis=0))
        return (state_f + summed + b_down).astype(jnp.bfloat16)
    outputs = lax.map(block_rows, (query_blocks, residual_blocks, starts))
    return outputs.reshape(SLOTS, width)

def reference(queries, new_kv, cache_kv, residual, prefix_len, dest_map, w_out, b_out, ln_gain, ln_bias, w_up, b_up, w_down, b_down):
    down_blocks = w_down.astype(jnp.float32).reshape(N_TOK, FF // N_TOK, D)

    def per_request(item):
        return one_request(item, w_out, b_out, ln_gain, ln_bias, w_up, b_up, down_blocks, b_down)
    outputs = lax.map(per_request, (queries, new_kv, cache_kv, residual, prefix_len))
    flat_rows = outputs.reshape(REQS * SLOTS, D)
    target = dest_map.reshape(REQS * SLOTS)
    where_to = jnp.where(target >= 0, target, TOKENS).astype(jnp.int32)
    return jnp.zeros((TOKENS, D), jnp.bfloat16).at[where_to].set(flat_rows, mode='drop')
```

```python
import functools
import math

import jax
import jax.numpy as jnp
from jax import lax
from jax.experimental import pallas as pl
from jax.experimental.pallas import tpu as pltpu
from jax.sharding import PartitionSpec as P

TOK_DEV = 128


neg_large = -1e30
ln_eps = 1e-05


def flash_kernel(
    scal_ref,
    q_ref,
    ck_ref,
    nk_ref,
    o_ref,
    m_sc,
    l_sc,
    acc_sc,
    *,
    tq,
    tk,
    heads,
    head_dim,
    n_cache,
    n_req,
    scale,
):
    r = pl.program_id(0)
    qi = pl.program_id(1)
    ki = pl.program_id(2)
    prefix = scal_ref[r]
    live = scal_ref[n_req + r]
    base = scal_ref[2 * n_req]
    spt = tq // heads
    tile_lo = qi * spt
    tile_live = tile_lo < live
    q_lo = base + tile_lo
    q_hi = q_lo + spt - 1

    @pl.when(ki == 0)
    def _init():
        m_sc[...] = jnp.full(m_sc.shape, neg_large, jnp.float32)
        l_sc[...] = jnp.zeros(l_sc.shape, jnp.float32)
        acc_sc[...] = jnp.zeros(acc_sc.shape, jnp.float32)

    def step(kv_ref, mask_fn):
        kv = kv_ref[0]
        k = kv[:, :head_dim]
        v = kv[:, head_dim:]
        s = (
            lax.dot_general(
                q_ref[0], k, (((1,), (1,)), ((), ())), preferred_element_type=jnp.float32
            )
            * scale
        )
        mask = None
        if mask_fn is not None:
            mask = mask_fn()
            s = jnp.where(mask, s, neg_large)
        m_prev = m_sc[...]
        m_new = jnp.maximum(m_prev, jnp.max(s, axis=-1, keepdims=True))
        p = jnp.exp(s - m_new)
        if mask is not None:
            p = jnp.where(mask, p, 0.0)
        alpha = jnp.exp(m_prev - m_new)
        l_sc[...] = alpha * l_sc[...] + jnp.sum(p, axis=-1, keepdims=True)
        acc_sc[...] = alpha * acc_sc[...] + jnp.dot(
            p.astype(jnp.bfloat16), v, preferred_element_type=jnp.float32
        )
        m_sc[...] = m_new

    is_cache = ki < n_cache
    kc = ki * tk
    kn = (ki - n_cache) * tk
    run_cache = is_cache & tile_live & (kc < prefix)
    full_cache = kc + tk <= prefix
    run_new = jnp.logical_not(is_cache) & tile_live & (kn <= q_hi)
    full_new = kn + tk - 1 <= q_lo

    def cache_mask():
        col = lax.broadcasted_iota(jnp.int32, (tq, tk), 1) + kc
        return col < prefix

    def new_mask():
        col = lax.broadcasted_iota(jnp.int32, (tq, tk), 1) + kn
        row = lax.broadcasted_iota(jnp.int32, (tq, tk), 0) // heads + q_lo
        return col <= row

    @pl.when(run_cache & full_cache)
    def _c_full():
        step(ck_ref, None)

    @pl.when(run_cache & jnp.logical_not(full_cache))
    def _c_part():
        step(ck_ref, cache_mask)

    @pl.when(run_new & full_new)
    def _n_full():
        step(nk_ref, None)

    @pl.when(run_new & jnp.logical_not(full_new))
    def _n_part():
        step(nk_ref, new_mask)

    @pl.when(ki == pl.num_programs(2) - 1)
    def _fin():
        l = l_sc[...]
        safe = jnp.where(l > 0, l, 1.0)
        out = jnp.where(l > 0, acc_sc[...] / safe, 0.0)
        o_ref[0] = out.astype(o_ref.dtype)


def flash_attention(q, ck, nk, scal, heads, tq, tk):
    n_req, rows, head_dim = q.shape
    n_cache = ck.shape[1] // tk
    n_new = nk.shape[1] // tk
    spt = tq // heads
    scale = 1.0 / math.sqrt(head_dim)

    def q_map(r, qi, ki, s):
        return (r, qi, 0)

    def c_map(r, qi, ki, s):
        last = jnp.maximum((s[r] + tk - 1) // tk - 1, 0)
        return (r, jnp.minimum(ki, last), 0)

    def n_map(r, qi, ki, s):
        q_hi = s[2 * n_req] + (qi + 1) * spt - 1
        last = jnp.minimum(q_hi // tk, n_new - 1)
        return (r, jnp.clip(ki - n_cache, 0, last), 0)

    kernel = functools.partial(
        flash_kernel,
        tq=tq,
        tk=tk,
        heads=heads,
        head_dim=head_dim,
        n_cache=n_cache,
        n_req=n_req,
        scale=scale,
    )
    grid_spec = pltpu.PrefetchScalarGridSpec(
        num_scalar_prefetch=1,
        grid=(n_req, rows // tq, n_cache + n_new),
        in_specs=[
            pl.BlockSpec((1, tq, head_dim), q_map),
            pl.BlockSpec((1, tk, ck.shape[2]), c_map),
            pl.BlockSpec((1, tk, nk.shape[2]), n_map),
        ],
        out_specs=pl.BlockSpec((1, tq, head_dim), q_map),
        scratch_shapes=[
            pltpu.VMEM((tq, 1), jnp.float32),
            pltpu.VMEM((tq, 1), jnp.float32),
            pltpu.VMEM((tq, head_dim), jnp.float32),
        ],
    )
    return pl.pallas_call(
        kernel,
        grid_spec=grid_spec,
        out_shape=jax.ShapeDtypeStruct((n_req, rows, head_dim), jnp.bfloat16),
    )(scal, q, ck, nk)


def per_device(
    queries,
    new_kv,
    cache_kv,
    residual,
    prefix_len,
    dest_map,
    w_out,
    b_out,
    ln_gain,
    ln_bias,
    w_up,
    b_up,
    w_down,
    b_down,
):
    group = lax.axis_index("req")
    member = lax.axis_index("tok")
    n_group = lax.axis_size("req")
    n_member = lax.axis_size("tok")
    devices = n_group * n_member
    req_dev, slot_dev, width = queries.shape
    head_dim = new_kv.shape[2] // 2
    heads = width // head_dim
    own_prefix = lax.dynamic_slice_in_dim(prefix_len, group * req_dev, req_dev)
    live_count = jnp.sum((dest_map >= 0).astype(jnp.int32), axis=1)
    base = (member * slot_dev).astype(jnp.int32)
    rows = slot_dev * heads
    tq = min(1024, rows)
    tk = 512
    q_flat = queries.reshape(req_dev, rows, head_dim)

    outs = []
    for r in range(req_dev):
        ck = lax.all_gather(cache_kv[r], "tok", axis=0, tiled=True)
        nk = lax.all_gather(new_kv[r], "tok", axis=0, tiled=True)
        scal = jnp.stack([own_prefix[r], live_count[r], base]).astype(jnp.int32)
        outs.append(
            flash_attention(q_flat[r : r + 1], ck[None], nk[None], scal, heads, tq, tk)
        )
    attended = jnp.concatenate(outs, axis=0)
    slots = req_dev * slot_dev
    attended = attended.reshape(slots, width)
    residual_flat = residual.reshape(slots, width)
    hidden_all = (
        residual_flat.astype(jnp.float32)
        + jnp.dot(attended, w_out, preferred_element_type=jnp.float32)
        + b_out
    ).astype(jnp.bfloat16)

    capacity = (slots + devices - 1) // devices
    target = dest_map.reshape(slots)
    is_live = target >= 0
    peer = jnp.where(is_live, target // TOK_DEV, devices)
    onehot = (peer[:, None] == jnp.arange(devices, dtype=jnp.int32)[None, :]).astype(jnp.int32)
    position = jnp.sum((jnp.cumsum(onehot, axis=0) - 1) * onehot, axis=1)
    where_to = jnp.where(is_live, peer * capacity + position, devices * capacity)
    send_slots = devices * capacity
    pick = (
        where_to[None, :] == jnp.arange(send_slots, dtype=jnp.int32)[:, None]
    ).astype(jnp.bfloat16)
    send_rows = jnp.dot(pick, hidden_all, preferred_element_type=jnp.float32).astype(
        jnp.bfloat16
    )
    row_ids = jnp.sum(
        jnp.where(
            where_to[None, :] == jnp.arange(send_slots, dtype=jnp.int32)[:, None],
            (target % TOK_DEV)[None, :] + 1,
            0,
        ),
        axis=1,
    ) - 1
    rows_in = lax.all_to_all(
        send_rows.reshape(devices, capacity, width),
        ("req", "tok"),
        split_axis=0,
        concat_axis=0,
        tiled=True,
    ).reshape(send_slots, width)
    ids_in = lax.all_to_all(
        row_ids.reshape(devices, capacity),
        ("req", "tok"),
        split_axis=0,
        concat_axis=0,
        tiled=True,
    ).reshape(send_slots)
    land = (ids_in[None, :] == jnp.arange(TOK_DEV, dtype=jnp.int32)[:, None]).astype(
        jnp.bfloat16
    )
    hidden_state = jnp.dot(land, rows_in, preferred_element_type=jnp.float32).astype(
        jnp.bfloat16
    )
    state_f = hidden_state.astype(jnp.float32)
    mean = jnp.mean(state_f, axis=-1, keepdims=True)
    centered = state_f - mean
    variance = jnp.mean(centered * centered, axis=-1, keepdims=True)
    normed = (centered * lax.rsqrt(variance + ln_eps) * ln_gain + ln_bias).astype(jnp.bfloat16)
    units = jax.nn.gelu(
        jnp.dot(
            lax.all_gather(normed, "tok", axis=0, tiled=True),
            w_up,
            preferred_element_type=jnp.float32,
        )
        + b_up,
        approximate=True,
    )
    terms = jnp.dot(units.astype(jnp.bfloat16), w_down, preferred_element_type=jnp.float32)
    summed = lax.psum_scatter(
        terms.astype(jnp.bfloat16), "tok", scatter_dimension=0, tiled=True
    ).astype(jnp.float32)
    return (state_f + summed + b_down).astype(jnp.bfloat16)


def solution(mesh):
    in_specs = (
        P("req", "tok", None),
        P("req", "tok", None),
        P("req", "tok", None),
        P("req", "tok", None),
        P(),
        P("req", "tok"),
        P(),
        P(),
        P(),
        P(),
        P(None, "tok"),
        P("tok"),
        P("tok", None),
        P(),
    )
    out_specs = P(("req", "tok"), None)
    return jax.shard_map(
        per_device, mesh=mesh, in_specs=in_specs, out_specs=out_specs, check_vma=False
    )
```

```python
import functools
import math

import jax
import jax.numpy as jnp
from jax import lax
from jax.experimental import pallas as pl
from jax.experimental.pallas import tpu as pltpu
from jax.sharding import PartitionSpec as P

TOK_DEV = 128


neg_large = -1e30
ln_eps = 1e-05


def flash_kernel(
    scal_ref,
    q_ref,
    ck_ref,
    cv_ref,
    nk_ref,
    nv_ref,
    o_ref,
    m_sc,
    l_sc,
    acc_sc,
    *,
    tq,
    tk,
    heads,
    n_cache,
    n_req,
    scale,
):
    r = pl.program_id(0)
    qi = pl.program_id(1)
    ki = pl.program_id(2)
    prefix = scal_ref[r]
    live = scal_ref[n_req + r]
    base = scal_ref[2 * n_req]
    spt = tq // heads
    tile_lo = qi * spt
    tile_live = tile_lo < live
    q_lo = base + tile_lo
    q_hi = q_lo + spt - 1

    @pl.when(ki == 0)
    def _init():
        m_sc[...] = jnp.full(m_sc.shape, neg_large, jnp.float32)
        l_sc[...] = jnp.zeros(l_sc.shape, jnp.float32)
        acc_sc[...] = jnp.zeros(acc_sc.shape, jnp.float32)

    def step(k_ref, v_ref, mask_fn):
        s = (
            lax.dot_general(
                k_ref[0], q_ref[0], (((1,), (1,)), ((), ())), preferred_element_type=jnp.float32
            )
            * scale
        )
        mask = None
        if mask_fn is not None:
            mask = mask_fn()
            s = jnp.where(mask, s, neg_large)
        m_prev = m_sc[...]
        m_new = jnp.maximum(m_prev, jnp.max(s, axis=0, keepdims=True))
        p = jnp.exp(s - m_new)
        if mask is not None:
            p = jnp.where(mask, p, 0.0)
        alpha = jnp.exp(m_prev - m_new)
        l_sc[...] = alpha * l_sc[...] + jnp.sum(p, axis=0, keepdims=True)
        acc_sc[...] = alpha * acc_sc[...] + jnp.dot(
            v_ref[0], p.astype(jnp.bfloat16), preferred_element_type=jnp.float32
        )
        m_sc[...] = m_new

    is_cache = ki < n_cache
    kc = ki * tk
    kn = (ki - n_cache) * tk
    run_cache = is_cache & tile_live & (kc < prefix)
    full_cache = kc + tk <= prefix
    run_new = jnp.logical_not(is_cache) & tile_live & (kn <= q_hi)
    full_new = kn + tk - 1 <= q_lo

    def cache_mask():
        key = lax.broadcasted_iota(jnp.int32, (tk, tq), 0) + kc
        return key < prefix

    def new_mask():
        key = lax.broadcasted_iota(jnp.int32, (tk, tq), 0) + kn
        slot = lax.broadcasted_iota(jnp.int32, (tk, tq), 1) // heads + q_lo
        return key <= slot

    @pl.when(run_cache & full_cache)
    def _c_full():
        step(ck_ref, cv_ref, None)

    @pl.when(run_cache & jnp.logical_not(full_cache))
    def _c_part():
        step(ck_ref, cv_ref, cache_mask)

    @pl.when(run_new & full_new)
    def _n_full():
        step(nk_ref, nv_ref, None)

    @pl.when(run_new & jnp.logical_not(full_new))
    def _n_part():
        step(nk_ref, nv_ref, new_mask)

    @pl.when(ki == pl.num_programs(2) - 1)
    def _fin():
        l = l_sc[...]
        safe = jnp.where(l > 0, l, 1.0)
        out = jnp.where(l > 0, acc_sc[...] / safe, 0.0)
        o_ref[0] = jnp.transpose(out).astype(o_ref.dtype)


def flash_attention(q, ckv, nkv, scal, heads, tq, tk):
    n_req, rows, head_dim = q.shape
    n_cache = ckv.shape[1] // tk
    n_new = nkv.shape[1] // tk
    spt = tq // heads
    scale = 1.0 / math.sqrt(head_dim)
    cvt = jnp.swapaxes(ckv[:, :, head_dim:], 1, 2)
    nvt = jnp.swapaxes(nkv[:, :, head_dim:], 1, 2)

    def q_map(r, qi, ki, s):
        return (r, qi, 0)

    def c_block(r, ki, s):
        last = jnp.maximum((s[r] + tk - 1) // tk - 1, 0)
        return jnp.minimum(ki, last)

    def n_block(r, qi, ki, s):
        q_hi = s[2 * n_req] + (qi + 1) * spt - 1
        last = jnp.minimum(q_hi // tk, n_new - 1)
        return jnp.clip(ki - n_cache, 0, last)

    kernel = functools.partial(
        flash_kernel,
        tq=tq,
        tk=tk,
        heads=heads,
        n_cache=n_cache,
        n_req=n_req,
        scale=scale,
    )
    grid_spec = pltpu.PrefetchScalarGridSpec(
        num_scalar_prefetch=1,
        grid=(n_req, rows // tq, n_cache + n_new),
        in_specs=[
            pl.BlockSpec((1, tq, head_dim), q_map),
            pl.BlockSpec((1, tk, head_dim), lambda r, qi, ki, s: (r, c_block(r, ki, s), 0)),
            pl.BlockSpec((1, head_dim, tk), lambda r, qi, ki, s: (r, 0, c_block(r, ki, s))),
            pl.BlockSpec((1, tk, head_dim), lambda r, qi, ki, s: (r, n_block(r, qi, ki, s), 0)),
            pl.BlockSpec((1, head_dim, tk), lambda r, qi, ki, s: (r, 0, n_block(r, qi, ki, s))),
        ],
        out_specs=pl.BlockSpec((1, tq, head_dim), q_map),
        scratch_shapes=[
            pltpu.VMEM((1, tq), jnp.float32),
            pltpu.VMEM((1, tq), jnp.float32),
            pltpu.VMEM((head_dim, tq), jnp.float32),
        ],
    )
    return pl.pallas_call(
        kernel,
        grid_spec=grid_spec,
        out_shape=jax.ShapeDtypeStruct((n_req, rows, head_dim), jnp.bfloat16),
    )(scal, q, ckv, cvt, nkv, nvt)


def per_device(
    queries,
    new_kv,
    cache_kv,
    residual,
    prefix_len,
    dest_map,
    w_out,
    b_out,
    ln_gain,
    ln_bias,
    w_up,
    b_up,
    w_down,
    b_down,
):
    group = lax.axis_index("req")
    member = lax.axis_index("tok")
    n_group = lax.axis_size("req")
    n_member = lax.axis_size("tok")
    devices = n_group * n_member
    req_dev, slot_dev, width = queries.shape
    head_dim = new_kv.shape[2] // 2
    heads = width // head_dim
    own_prefix = lax.dynamic_slice_in_dim(prefix_len, group * req_dev, req_dev)
    live_count = jnp.sum((dest_map >= 0).astype(jnp.int32), axis=1)
    base = (member * slot_dev).astype(jnp.int32)
    rows = slot_dev * heads
    tq = min(1024, rows)
    tk = 512
    q_flat = queries.reshape(req_dev, rows, head_dim)

    outs = []
    for r in range(req_dev):
        ck = lax.all_gather(cache_kv[r], "tok", axis=0, tiled=True)
        nk = lax.all_gather(new_kv[r], "tok", axis=0, tiled=True)
        scal = jnp.stack([own_prefix[r], live_count[r], base]).astype(jnp.int32)
        outs.append(
            flash_attention(q_flat[r : r + 1], ck[None], nk[None], scal, heads, tq, tk)
        )
    attended = jnp.concatenate(outs, axis=0)
    slots = req_dev * slot_dev
    attended = attended.reshape(slots, width)
    residual_flat = residual.reshape(slots, width)
    hidden_all = (
        residual_flat.astype(jnp.float32)
        + jnp.dot(attended, w_out, preferred_element_type=jnp.float32)
        + b_out
    ).astype(jnp.bfloat16)

    capacity = (slots + devices - 1) // devices
    target = dest_map.reshape(slots)
    is_live = target >= 0
    peer = jnp.where(is_live, target // TOK_DEV, devices)
    onehot = (peer[:, None] == jnp.arange(devices, dtype=jnp.int32)[None, :]).astype(jnp.int32)
    position = jnp.sum((jnp.cumsum(onehot, axis=0) - 1) * onehot, axis=1)
    where_to = jnp.where(is_live, peer * capacity + position, devices * capacity)
    send_slots = devices * capacity
    pick = (
        where_to[None, :] == jnp.arange(send_slots, dtype=jnp.int32)[:, None]
    ).astype(jnp.bfloat16)
    send_rows = jnp.dot(pick, hidden_all, preferred_element_type=jnp.float32).astype(
        jnp.bfloat16
    )
    row_ids = jnp.sum(
        jnp.where(
            where_to[None, :] == jnp.arange(send_slots, dtype=jnp.int32)[:, None],
            (target % TOK_DEV)[None, :] + 1,
            0,
        ),
        axis=1,
    ) - 1
    rows_in = lax.all_to_all(
        send_rows.reshape(devices, capacity, width),
        ("req", "tok"),
        split_axis=0,
        concat_axis=0,
        tiled=True,
    ).reshape(send_slots, width)
    ids_in = lax.all_to_all(
        row_ids.reshape(devices, capacity),
        ("req", "tok"),
        split_axis=0,
        concat_axis=0,
        tiled=True,
    ).reshape(send_slots)
    land = (ids_in[None, :] == jnp.arange(TOK_DEV, dtype=jnp.int32)[:, None]).astype(
        jnp.bfloat16
    )
    hidden_state = jnp.dot(land, rows_in, preferred_element_type=jnp.float32).astype(
        jnp.bfloat16
    )
    state_f = hidden_state.astype(jnp.float32)
    mean = jnp.mean(state_f, axis=-1, keepdims=True)
    centered = state_f - mean
    variance = jnp.mean(centered * centered, axis=-1, keepdims=True)
    normed = (centered * lax.rsqrt(variance + ln_eps) * ln_gain + ln_bias).astype(jnp.bfloat16)
    units = jax.nn.gelu(
        jnp.dot(
            lax.all_gather(normed, "tok", axis=0, tiled=True),
            w_up,
            preferred_element_type=jnp.float32,
        )
        + b_up,
        approximate=True,
    )
    terms = jnp.dot(units.astype(jnp.bfloat16), w_down, preferred_element_type=jnp.float32)
    summed = lax.psum_scatter(
        terms.astype(jnp.bfloat16), "tok", scatter_dimension=0, tiled=True
    ).astype(jnp.float32)
    return (state_f + summed + b_down).astype(jnp.bfloat16)


def solution(mesh):
    in_specs = (
        P("req", "tok", None),
        P("req", "tok", None),
        P("req", "tok", None),
        P("req", "tok", None),
        P(),
        P("req", "tok"),
        P(),
        P(),
        P(),
        P(),
        P(None, "tok"),
        P("tok"),
        P("tok", None),
        P(),
    )
    out_specs = P(("req", "tok"), None)
    return jax.shard_map(
        per_device, mesh=mesh, in_specs=in_specs, out_specs=out_specs, check_vma=False
    )
```

```python
import functools
import math

import jax
import jax.numpy as jnp
from jax import lax
from jax.experimental import pallas as pl
from jax.experimental.pallas import tpu as pltpu
from jax.sharding import PartitionSpec as P

TOK_DEV = 128


neg_large = -1e30
ln_eps = 1e-05


def flash_kernel(
    scal_ref,
    q_ref,
    ck_ref,
    cv_ref,
    nk_ref,
    nv_ref,
    o_ref,
    m_sc,
    l_sc,
    acc_sc,
    *,
    tq,
    tk,
    heads,
    n_cache,
    n_req,
    scale,
):
    r = pl.program_id(0)
    qi = pl.program_id(1)
    ki = pl.program_id(2)
    prefix = scal_ref[r]
    live = scal_ref[n_req + r]
    base = scal_ref[2 * n_req]
    spt = tq // heads
    tile_lo = qi * spt
    tile_live = tile_lo < live
    q_lo = base + tile_lo
    q_hi = q_lo + spt - 1

    @pl.when(ki == 0)
    def _init():
        m_sc[...] = jnp.full(m_sc.shape, neg_large, jnp.float32)
        l_sc[...] = jnp.zeros(l_sc.shape, jnp.float32)
        acc_sc[...] = jnp.zeros(acc_sc.shape, jnp.float32)

    def step(k_ref, v_ref, mask_fn):
        s = (
            lax.dot_general(
                k_ref[0], q_ref[0], (((1,), (1,)), ((), ())), preferred_element_type=jnp.float32
            )
            * scale
        )
        mask = None
        if mask_fn is not None:
            mask = mask_fn()
            s = jnp.where(mask, s, neg_large)
        m_prev = m_sc[...]
        m_new = jnp.maximum(m_prev, jnp.max(s, axis=0, keepdims=True))
        p = jnp.exp(s - m_new)
        if mask is not None:
            p = jnp.where(mask, p, 0.0)
        alpha = jnp.exp(m_prev - m_new)
        l_sc[...] = alpha * l_sc[...] + jnp.sum(p, axis=0, keepdims=True)
        acc_sc[...] = alpha * acc_sc[...] + jnp.dot(
            v_ref[0], p.astype(jnp.bfloat16), preferred_element_type=jnp.float32
        )
        m_sc[...] = m_new

    is_cache = ki < n_cache
    kc = ki * tk
    kn = (ki - n_cache) * tk
    run_cache = is_cache & tile_live & (kc < prefix)
    full_cache = kc + tk <= prefix
    run_new = jnp.logical_not(is_cache) & tile_live & (kn <= q_hi)
    full_new = kn + tk - 1 <= q_lo

    def cache_mask():
        key = lax.broadcasted_iota(jnp.int32, (tk, tq), 0) + kc
        return key < prefix

    def new_mask():
        key = lax.broadcasted_iota(jnp.int32, (tk, tq), 0) + kn
        slot = lax.broadcasted_iota(jnp.int32, (tk, tq), 1) // heads + q_lo
        return key <= slot

    @pl.when(run_cache & full_cache)
    def _c_full():
        step(ck_ref, cv_ref, None)

    @pl.when(run_cache & jnp.logical_not(full_cache))
    def _c_part():
        step(ck_ref, cv_ref, cache_mask)

    @pl.when(run_new & full_new)
    def _n_full():
        step(nk_ref, nv_ref, None)

    @pl.when(run_new & jnp.logical_not(full_new))
    def _n_part():
        step(nk_ref, nv_ref, new_mask)

    @pl.when(ki == pl.num_programs(2) - 1)
    def _fin():
        l = l_sc[...]
        safe = jnp.where(l > 0, l, 1.0)
        out = jnp.where(l > 0, acc_sc[...] / safe, 0.0)
        o_ref[0] = jnp.transpose(out).astype(o_ref.dtype)


def flash_attention(q, ckv, nkv, scal, heads, tq, tk):
    n_req, rows, head_dim = q.shape
    n_cache = ckv.shape[1] // tk
    n_new = nkv.shape[1] // tk
    spt = tq // heads
    scale = 1.0 / math.sqrt(head_dim)
    cvt = jnp.swapaxes(ckv[:, :, head_dim:], 1, 2)
    nvt = jnp.swapaxes(nkv[:, :, head_dim:], 1, 2)

    def q_map(r, qi, ki, s):
        return (r, qi, 0)

    def c_block(r, ki, s):
        last = jnp.maximum((s[r] + tk - 1) // tk - 1, 0)
        return jnp.minimum(ki, last)

    def n_block(r, qi, ki, s):
        q_hi = s[2 * n_req] + (qi + 1) * spt - 1
        last = jnp.minimum(q_hi // tk, n_new - 1)
        return jnp.clip(ki - n_cache, 0, last)

    kernel = functools.partial(
        flash_kernel,
        tq=tq,
        tk=tk,
        heads=heads,
        n_cache=n_cache,
        n_req=n_req,
        scale=scale,
    )
    grid_spec = pltpu.PrefetchScalarGridSpec(
        num_scalar_prefetch=1,
        grid=(n_req, rows // tq, n_cache + n_new),
        in_specs=[
            pl.BlockSpec((1, tq, head_dim), q_map),
            pl.BlockSpec((1, tk, head_dim), lambda r, qi, ki, s: (r, c_block(r, ki, s), 0)),
            pl.BlockSpec((1, head_dim, tk), lambda r, qi, ki, s: (r, 0, c_block(r, ki, s))),
            pl.BlockSpec((1, tk, head_dim), lambda r, qi, ki, s: (r, n_block(r, qi, ki, s), 0)),
            pl.BlockSpec((1, head_dim, tk), lambda r, qi, ki, s: (r, 0, n_block(r, qi, ki, s))),
        ],
        out_specs=pl.BlockSpec((1, tq, head_dim), q_map),
        scratch_shapes=[
            pltpu.VMEM((1, tq), jnp.float32),
            pltpu.VMEM((1, tq), jnp.float32),
            pltpu.VMEM((head_dim, tq), jnp.float32),
        ],
    )
    return pl.pallas_call(
        kernel,
        grid_spec=grid_spec,
        out_shape=jax.ShapeDtypeStruct((n_req, rows, head_dim), jnp.bfloat16),
    )(scal, q, ckv, cvt, nkv, nvt)


def per_device(
    queries,
    new_kv,
    cache_kv,
    residual,
    prefix_len,
    dest_map,
    w_out,
    b_out,
    ln_gain,
    ln_bias,
    w_up,
    b_up,
    w_down,
    b_down,
):
    group = lax.axis_index("req")
    member = lax.axis_index("tok")
    n_group = lax.axis_size("req")
    n_member = lax.axis_size("tok")
    devices = n_group * n_member
    req_dev, slot_dev, width = queries.shape
    head_dim = new_kv.shape[2] // 2
    heads = width // head_dim
    own_prefix = lax.dynamic_slice_in_dim(prefix_len, group * req_dev, req_dev)
    live_count = jnp.sum((dest_map >= 0).astype(jnp.int32), axis=1)
    base = (member * slot_dev).astype(jnp.int32)
    rows = slot_dev * heads
    tq = min(1024, rows)
    tk = 512
    q_flat = queries.reshape(req_dev, rows, head_dim)

    prefix_dev = cache_kv.shape[1]
    local_kv = jnp.concatenate([cache_kv, new_kv], axis=1)
    gathered = [lax.all_gather(local_kv[0], "tok", axis=0, tiled=True)]
    for r in range(1, req_dev):
        mine, gathered[-1] = lax.optimization_barrier((local_kv[r], gathered[-1]))
        gathered.append(lax.all_gather(mine, "tok", axis=0, tiled=True))
    outs = []
    for r in range(req_dev):
        both = gathered[r].reshape(n_member, prefix_dev + slot_dev, local_kv.shape[-1])
        ck = both[:, :prefix_dev].reshape(n_member * prefix_dev, local_kv.shape[-1])
        nk = both[:, prefix_dev:].reshape(n_member * slot_dev, local_kv.shape[-1])
        scal = jnp.stack([own_prefix[r], live_count[r], base]).astype(jnp.int32)
        outs.append(
            flash_attention(q_flat[r : r + 1], ck[None], nk[None], scal, heads, tq, tk)
        )
    attended = jnp.concatenate(outs, axis=0)
    slots = req_dev * slot_dev
    attended = attended.reshape(slots, width)
    residual_flat = residual.reshape(slots, width)
    hidden_all = (
        residual_flat.astype(jnp.float32)
        + jnp.dot(attended, w_out, preferred_element_type=jnp.float32)
        + b_out
    ).astype(jnp.bfloat16)

    capacity = (slots + devices - 1) // devices
    target = dest_map.reshape(slots)
    is_live = target >= 0
    peer = jnp.where(is_live, target // TOK_DEV, devices)
    onehot = (peer[:, None] == jnp.arange(devices, dtype=jnp.int32)[None, :]).astype(jnp.int32)
    position = jnp.sum((jnp.cumsum(onehot, axis=0) - 1) * onehot, axis=1)
    where_to = jnp.where(is_live, peer * capacity + position, devices * capacity)
    send_slots = devices * capacity
    pick = (
        where_to[None, :] == jnp.arange(send_slots, dtype=jnp.int32)[:, None]
    ).astype(jnp.bfloat16)
    send_rows = jnp.dot(pick, hidden_all, preferred_element_type=jnp.float32).astype(
        jnp.bfloat16
    )
    row_ids = jnp.sum(
        jnp.where(
            where_to[None, :] == jnp.arange(send_slots, dtype=jnp.int32)[:, None],
            (target % TOK_DEV)[None, :] + 1,
            0,
        ),
        axis=1,
    ) - 1
    rows_in = lax.all_to_all(
        send_rows.reshape(devices, capacity, width),
        ("req", "tok"),
        split_axis=0,
        concat_axis=0,
        tiled=True,
    ).reshape(send_slots, width)
    ids_in = lax.all_to_all(
        row_ids.reshape(devices, capacity),
        ("req", "tok"),
        split_axis=0,
        concat_axis=0,
        tiled=True,
    ).reshape(send_slots)
    land = (ids_in[None, :] == jnp.arange(TOK_DEV, dtype=jnp.int32)[:, None]).astype(
        jnp.bfloat16
    )
    hidden_state = jnp.dot(land, rows_in, preferred_element_type=jnp.float32).astype(
        jnp.bfloat16
    )
    state_f = hidden_state.astype(jnp.float32)
    mean = jnp.mean(state_f, axis=-1, keepdims=True)
    centered = state_f - mean
    variance = jnp.mean(centered * centered, axis=-1, keepdims=True)
    normed = (centered * lax.rsqrt(variance + ln_eps) * ln_gain + ln_bias).astype(jnp.bfloat16)
    units = jax.nn.gelu(
        jnp.dot(
            lax.all_gather(normed, "tok", axis=0, tiled=True),
            w_up,
            preferred_element_type=jnp.float32,
        )
        + b_up,
        approximate=True,
    )
    terms = jnp.dot(units.astype(jnp.bfloat16), w_down, preferred_element_type=jnp.float32)
    parts = lax.all_to_all(
        terms.astype(jnp.bfloat16).reshape(n_member, TOK_DEV, width),
        "tok",
        split_axis=0,
        concat_axis=0,
        tiled=True,
    )
    summed = jnp.sum(parts.astype(jnp.float32), axis=0)
    return (state_f + summed + b_down).astype(jnp.bfloat16)


def solution(mesh):
    in_specs = (
        P("req", "tok", None),
        P("req", "tok", None),
        P("req", "tok", None),
        P("req", "tok", None),
        P(),
        P("req", "tok"),
        P(),
        P(),
        P(),
        P(),
        P(None, "tok"),
        P("tok"),
        P("tok", None),
        P(),
    )
    out_specs = P(("req", "tok"), None)
    return jax.shard_map(
        per_device, mesh=mesh, in_specs=in_specs, out_specs=out_specs, check_vma=False
    )
```

```python
import functools
import math

import jax
import jax.numpy as jnp
from jax import lax
from jax.experimental import pallas as pl
from jax.experimental.pallas import tpu as pltpu
from jax.sharding import PartitionSpec as P

TOK_DEV = 128


neg_large = -1e30
ln_eps = 1e-05


def flash_kernel(
    scal_ref,
    q_ref,
    ck_ref,
    cv_ref,
    nk_ref,
    nv_ref,
    o_ref,
    m_sc,
    acc_sc,
    *,
    tq,
    head_dim,
    tk,
    heads,
    n_cache,
    n_req,
    scale,
):
    r = pl.program_id(0)
    qi = pl.program_id(1)
    ki = pl.program_id(2)
    prefix = scal_ref[r]
    live = scal_ref[n_req + r]
    base = scal_ref[2 * n_req]
    spt = tq // heads
    tile_lo = qi * spt
    tile_live = tile_lo < live
    q_lo = base + tile_lo
    q_hi = q_lo + spt - 1

    @pl.when(ki == 0)
    def _init():
        m_sc[...] = jnp.full(m_sc.shape, neg_large, jnp.float32)
        acc_sc[...] = jnp.zeros(acc_sc.shape, jnp.float32)

    def step(k_ref, v_ref, mask_fn):
        s = (
            lax.dot_general(
                k_ref[0], q_ref[0], (((1,), (1,)), ((), ())), preferred_element_type=jnp.float32
            )
            * scale
        )
        mask = None
        if mask_fn is not None:
            mask = mask_fn()
            s = jnp.where(mask, s, neg_large)
        m_prev = m_sc[...]
        m_new = jnp.maximum(m_prev, jnp.max(s, axis=0, keepdims=True))
        p = jnp.exp(s - m_new)
        if mask is not None:
            p = jnp.where(mask, p, 0.0)
        alpha = jnp.exp(m_prev - m_new)
        acc_sc[...] = alpha * acc_sc[...] + jnp.dot(
            v_ref[0], p.astype(jnp.bfloat16), preferred_element_type=jnp.float32
        )
        m_sc[...] = m_new

    is_cache = ki < n_cache
    kc = ki * tk
    kn = (ki - n_cache) * tk
    run_cache = is_cache & tile_live & (kc < prefix)
    full_cache = kc + tk <= prefix
    run_new = jnp.logical_not(is_cache) & tile_live & (kn <= q_hi)
    full_new = kn + tk - 1 <= q_lo

    def cache_mask():
        key = lax.broadcasted_iota(jnp.int32, (tk, tq), 0) + kc
        return key < prefix

    def new_mask():
        key = lax.broadcasted_iota(jnp.int32, (tk, tq), 0) + kn
        slot = lax.broadcasted_iota(jnp.int32, (tk, tq), 1) // heads + q_lo
        return key <= slot

    @pl.when(run_cache & full_cache)
    def _c_full():
        step(ck_ref, cv_ref, None)

    @pl.when(run_cache & jnp.logical_not(full_cache))
    def _c_part():
        step(ck_ref, cv_ref, cache_mask)

    @pl.when(run_new & full_new)
    def _n_full():
        step(nk_ref, nv_ref, None)

    @pl.when(run_new & jnp.logical_not(full_new))
    def _n_part():
        step(nk_ref, nv_ref, new_mask)

    @pl.when(ki == pl.num_programs(2) - 1)
    def _fin():
        acc = acc_sc[...]
        l = acc[head_dim : head_dim + 1]
        safe = jnp.where(l > 0, l, 1.0)
        out = jnp.where(l > 0, acc[:head_dim] / safe, 0.0)
        o_ref[0] = jnp.transpose(out).astype(o_ref.dtype)


def flash_attention(q, ckv, nkv, scal, heads, tq, tk):
    n_req, rows, head_dim = q.shape
    n_cache = ckv.shape[1] // tk
    n_new = nkv.shape[1] // tk
    spt = tq // heads
    scale = 1.0 / math.sqrt(head_dim)
    ones = jnp.ones((n_req, 8, 1), jnp.bfloat16)
    cvt = jnp.swapaxes(ckv[:, :, head_dim:], 1, 2)
    cvt = jnp.concatenate([cvt, jnp.broadcast_to(ones, (n_req, 8, cvt.shape[2]))], axis=1)
    nvt = jnp.swapaxes(nkv[:, :, head_dim:], 1, 2)
    nvt = jnp.concatenate([nvt, jnp.broadcast_to(ones, (n_req, 8, nvt.shape[2]))], axis=1)
    ext = head_dim + 8

    def q_map(r, qi, ki, s):
        return (r, qi, 0)

    def c_block(r, ki, s):
        last = jnp.maximum((s[r] + tk - 1) // tk - 1, 0)
        return jnp.minimum(ki, last)

    def n_block(r, qi, ki, s):
        q_hi = s[2 * n_req] + (qi + 1) * spt - 1
        last = jnp.minimum(q_hi // tk, n_new - 1)
        return jnp.clip(ki - n_cache, 0, last)

    kernel = functools.partial(
        flash_kernel,
        tq=tq,
        tk=tk,
        heads=heads,
        head_dim=head_dim,
        n_cache=n_cache,
        n_req=n_req,
        scale=scale,
    )
    grid_spec = pltpu.PrefetchScalarGridSpec(
        num_scalar_prefetch=1,
        grid=(n_req, rows // tq, n_cache + n_new),
        in_specs=[
            pl.BlockSpec((1, tq, head_dim), q_map),
            pl.BlockSpec((1, tk, head_dim), lambda r, qi, ki, s: (r, c_block(r, ki, s), 0)),
            pl.BlockSpec((1, ext, tk), lambda r, qi, ki, s: (r, 0, c_block(r, ki, s))),
            pl.BlockSpec((1, tk, head_dim), lambda r, qi, ki, s: (r, n_block(r, qi, ki, s), 0)),
            pl.BlockSpec((1, ext, tk), lambda r, qi, ki, s: (r, 0, n_block(r, qi, ki, s))),
        ],
        out_specs=pl.BlockSpec((1, tq, head_dim), q_map),
        scratch_shapes=[
            pltpu.VMEM((1, tq), jnp.float32),
            pltpu.VMEM((ext, tq), jnp.float32),
        ],
    )
    return pl.pallas_call(
        kernel,
        grid_spec=grid_spec,
        out_shape=jax.ShapeDtypeStruct((n_req, rows, head_dim), jnp.bfloat16),
    )(scal, q, ckv, cvt, nkv, nvt)


def per_device(
    queries,
    new_kv,
    cache_kv,
    residual,
    prefix_len,
    dest_map,
    w_out,
    b_out,
    ln_gain,
    ln_bias,
    w_up,
    b_up,
    w_down,
    b_down,
):
    group = lax.axis_index("req")
    member = lax.axis_index("tok")
    n_group = lax.axis_size("req")
    n_member = lax.axis_size("tok")
    devices = n_group * n_member
    req_dev, slot_dev, width = queries.shape
    head_dim = new_kv.shape[2] // 2
    heads = width // head_dim
    own_prefix = lax.dynamic_slice_in_dim(prefix_len, group * req_dev, req_dev)
    live_count = jnp.sum((dest_map >= 0).astype(jnp.int32), axis=1)
    base = (member * slot_dev).astype(jnp.int32)
    rows = slot_dev * heads
    tq = min(2048, rows)
    tk = 1024
    q_flat = queries.reshape(req_dev, rows, head_dim)

    prefix_dev = cache_kv.shape[1]
    local_kv = jnp.concatenate([cache_kv, new_kv], axis=1)
    gathered = [lax.all_gather(local_kv[0], "tok", axis=0, tiled=True)]
    for r in range(1, req_dev):
        mine, gathered[-1] = lax.optimization_barrier((local_kv[r], gathered[-1]))
        gathered.append(lax.all_gather(mine, "tok", axis=0, tiled=True))
    outs = []
    for r in range(req_dev):
        both = gathered[r].reshape(n_member, prefix_dev + slot_dev, local_kv.shape[-1])
        ck = both[:, :prefix_dev].reshape(n_member * prefix_dev, local_kv.shape[-1])
        nk = both[:, prefix_dev:].reshape(n_member * slot_dev, local_kv.shape[-1])
        scal = jnp.stack([own_prefix[r], live_count[r], base]).astype(jnp.int32)
        outs.append(
            flash_attention(q_flat[r : r + 1], ck[None], nk[None], scal, heads, tq, tk)
        )
    attended = jnp.concatenate(outs, axis=0)
    slots = req_dev * slot_dev
    attended = attended.reshape(slots, width)
    residual_flat = residual.reshape(slots, width)
    hidden_all = (
        residual_flat.astype(jnp.float32)
        + jnp.dot(attended, w_out, preferred_element_type=jnp.float32)
        + b_out
    ).astype(jnp.bfloat16)

    capacity = (slots + devices - 1) // devices
    target = dest_map.reshape(slots)
    is_live = target >= 0
    peer = jnp.where(is_live, target // TOK_DEV, devices)
    onehot = (peer[:, None] == jnp.arange(devices, dtype=jnp.int32)[None, :]).astype(jnp.int32)
    position = jnp.sum((jnp.cumsum(onehot, axis=0) - 1) * onehot, axis=1)
    where_to = jnp.where(is_live, peer * capacity + position, devices * capacity)
    send_slots = devices * capacity
    pick = (
        where_to[None, :] == jnp.arange(send_slots, dtype=jnp.int32)[:, None]
    ).astype(jnp.bfloat16)
    send_rows = jnp.dot(pick, hidden_all, preferred_element_type=jnp.float32).astype(
        jnp.bfloat16
    )
    row_ids = jnp.sum(
        jnp.where(
            where_to[None, :] == jnp.arange(send_slots, dtype=jnp.int32)[:, None],
            (target % TOK_DEV)[None, :] + 1,
            0,
        ),
        axis=1,
    ) - 1
    rows_in = lax.all_to_all(
        send_rows.reshape(devices, capacity, width),
        ("req", "tok"),
        split_axis=0,
        concat_axis=0,
        tiled=True,
    ).reshape(send_slots, width)
    ids_in = lax.all_to_all(
        row_ids.reshape(devices, capacity),
        ("req", "tok"),
        split_axis=0,
        concat_axis=0,
        tiled=True,
    ).reshape(send_slots)
    land = (ids_in[None, :] == jnp.arange(TOK_DEV, dtype=jnp.int32)[:, None]).astype(
        jnp.bfloat16
    )
    hidden_state = jnp.dot(land, rows_in, preferred_element_type=jnp.float32).astype(
        jnp.bfloat16
    )
    state_f = hidden_state.astype(jnp.float32)
    mean = jnp.mean(state_f, axis=-1, keepdims=True)
    centered = state_f - mean
    variance = jnp.mean(centered * centered, axis=-1, keepdims=True)
    normed = (centered * lax.rsqrt(variance + ln_eps) * ln_gain + ln_bias).astype(jnp.bfloat16)
    units = jax.nn.gelu(
        jnp.dot(
            lax.all_gather(normed, "tok", axis=0, tiled=True),
            w_up,
            preferred_element_type=jnp.float32,
        )
        + b_up,
        approximate=True,
    )
    terms = jnp.dot(units.astype(jnp.bfloat16), w_down, preferred_element_type=jnp.float32)
    summed = lax.psum_scatter(
        terms.astype(jnp.bfloat16), "tok", scatter_dimension=0, tiled=True
    ).astype(jnp.float32)
    return (state_f + summed + b_down).astype(jnp.bfloat16)


def solution(mesh):
    in_specs = (
        P("req", "tok", None),
        P("req", "tok", None),
        P("req", "tok", None),
        P("req", "tok", None),
        P(),
        P("req", "tok"),
        P(),
        P(),
        P(),
        P(),
        P(None, "tok"),
        P("tok"),
        P("tok", None),
        P(),
    )
    out_specs = P(("req", "tok"), None)
    return jax.shard_map(
        per_device, mesh=mesh, in_specs=in_specs, out_specs=out_specs, check_vma=False
    )
```

```python
import functools
import math

import jax
import jax.numpy as jnp
from jax import lax
from jax.experimental import pallas as pl
from jax.experimental.pallas import tpu as pltpu
from jax.sharding import PartitionSpec as P

TOK_DEV = 128


neg_large = -1e30
ln_eps = 1e-05


def flash_kernel(
    scal_ref,
    q_ref,
    ck_ref,
    cv_ref,
    nk_ref,
    nv_ref,
    o_ref,
    m_sc,
    acc_sc,
    *,
    tq,
    tk,
    heads,
    head_dim,
    n_cache,
    scale,
):
    qi = pl.program_id(1)
    ki = pl.program_id(2)
    prefix = scal_ref[0]
    live = scal_ref[1]
    base = scal_ref[2]
    spt = tq // heads
    tile_lo = qi * spt
    tile_live = tile_lo < live
    q_lo = base + tile_lo
    q_hi = q_lo + spt - 1

    @pl.when(ki == 0)
    def _init():
        m_sc[...] = jnp.full(m_sc.shape, neg_large, jnp.float32)
        acc_sc[...] = jnp.zeros(acc_sc.shape, jnp.float32)

    def step(k_ref, v_ref, mask_fn):
        pieces, chunk = k_ref.shape[0], k_ref.shape[1]
        k = k_ref[...].reshape(pieces * chunk, head_dim)
        s = (
            lax.dot_general(
                k, q_ref[0], (((1,), (1,)), ((), ())), preferred_element_type=jnp.float32
            )
            * scale
        )
        mask = None
        if mask_fn is not None:
            mask = mask_fn()
            s = jnp.where(mask, s, neg_large)
        m_prev = m_sc[...]
        m_new = jnp.maximum(m_prev, jnp.max(s, axis=0, keepdims=True))
        p = jnp.exp(s - m_new)
        if mask is not None:
            p = jnp.where(mask, p, 0.0)
        alpha = jnp.exp(m_prev - m_new)
        pb = p.astype(jnp.bfloat16)
        total = alpha * acc_sc[...]
        for piece in range(pieces):
            total = total + jnp.dot(
                v_ref[piece],
                pb[piece * chunk : (piece + 1) * chunk],
                preferred_element_type=jnp.float32,
            )
        acc_sc[...] = total
        m_sc[...] = m_new

    is_cache = ki < n_cache
    kc = ki * tk
    kn = (ki - n_cache) * tk
    run_cache = is_cache & tile_live & (kc < prefix)
    full_cache = kc + tk <= prefix
    run_new = jnp.logical_not(is_cache) & tile_live & (kn <= q_hi)
    full_new = kn + tk - 1 <= q_lo

    def cache_mask():
        key = lax.broadcasted_iota(jnp.int32, (tk, tq), 0) + kc
        return key < prefix

    def new_mask():
        key = lax.broadcasted_iota(jnp.int32, (tk, tq), 0) + kn
        slot = lax.broadcasted_iota(jnp.int32, (tk, tq), 1) // heads + q_lo
        return key <= slot

    @pl.when(run_cache & full_cache)
    def _c_full():
        step(ck_ref, cv_ref, None)

    @pl.when(run_cache & jnp.logical_not(full_cache))
    def _c_part():
        step(ck_ref, cv_ref, cache_mask)

    @pl.when(run_new & full_new)
    def _n_full():
        step(nk_ref, nv_ref, None)

    @pl.when(run_new & jnp.logical_not(full_new))
    def _n_part():
        step(nk_ref, nv_ref, new_mask)

    @pl.when(ki == pl.num_programs(2) - 1)
    def _fin():
        acc = acc_sc[...]
        l = acc[head_dim : head_dim + 1]
        safe = jnp.where(l > 0, l, 1.0)
        out = jnp.where(l > 0, acc[:head_dim] / safe, 0.0)
        o_ref[0] = jnp.transpose(out).astype(o_ref.dtype)


def flash_attention(q, req, both, scal, heads, tq, tk, prefix_dev, slot_dev):
    n_req, rows, head_dim = q.shape
    n_member = both.shape[0]
    n_cache = n_member * prefix_dev // tk
    n_new = n_member * slot_dev // tk
    per_cache = tk // prefix_dev
    per_new = tk // slot_dev
    new_at = prefix_dev // slot_dev
    spt = tq // heads
    scale = 1.0 / math.sqrt(head_dim)
    ones = jnp.ones((n_member, 8, both.shape[1]), jnp.bfloat16)
    vt = jnp.concatenate([jnp.swapaxes(both[:, :, head_dim:], 1, 2), ones], axis=1)
    ext = head_dim + 8

    def q_map(r, qi, ki, s):
        return (req, qi, 0)

    def o_map(r, qi, ki, s):
        return (0, qi, 0)

    def c_block(ki, s):
        last = jnp.maximum((s[0] + tk - 1) // tk - 1, 0)
        return jnp.minimum(ki, last)

    def n_block(qi, ki, s):
        q_hi = s[2] + (qi + 1) * spt - 1
        last = jnp.minimum(q_hi // tk, n_new - 1)
        return jnp.clip(ki - n_cache, 0, last)

    kernel = functools.partial(
        flash_kernel,
        tq=tq,
        tk=tk,
        heads=heads,
        head_dim=head_dim,
        n_cache=n_cache,
        scale=scale,
    )
    grid_spec = pltpu.PrefetchScalarGridSpec(
        num_scalar_prefetch=1,
        grid=(1, rows // tq, n_cache + n_new),
        in_specs=[
            pl.BlockSpec((1, tq, head_dim), q_map),
            pl.BlockSpec(
                (per_cache, prefix_dev, head_dim),
                lambda r, qi, ki, s: (c_block(ki, s), 0, 0),
            ),
            pl.BlockSpec(
                (per_cache, ext, prefix_dev),
                lambda r, qi, ki, s: (c_block(ki, s), 0, 0),
            ),
            pl.BlockSpec(
                (per_new, slot_dev, head_dim),
                lambda r, qi, ki, s: (n_block(qi, ki, s), new_at, 0),
            ),
            pl.BlockSpec(
                (per_new, ext, slot_dev),
                lambda r, qi, ki, s: (n_block(qi, ki, s), 0, new_at),
            ),
        ],
        out_specs=pl.BlockSpec((1, tq, head_dim), o_map),
        scratch_shapes=[
            pltpu.VMEM((1, tq), jnp.float32),
            pltpu.VMEM((ext, tq), jnp.float32),
        ],
    )
    return pl.pallas_call(
        kernel,
        grid_spec=grid_spec,
        out_shape=jax.ShapeDtypeStruct((1, rows, head_dim), jnp.bfloat16),
    )(scal, q, both, vt, both, vt)


def per_device(
    queries,
    new_kv,
    cache_kv,
    residual,
    prefix_len,
    dest_map,
    w_out,
    b_out,
    ln_gain,
    ln_bias,
    w_up,
    b_up,
    w_down,
    b_down,
):
    group = lax.axis_index("req")
    member = lax.axis_index("tok")
    n_group = lax.axis_size("req")
    n_member = lax.axis_size("tok")
    devices = n_group * n_member
    req_dev, slot_dev, width = queries.shape
    head_dim = new_kv.shape[2] // 2
    heads = width // head_dim
    own_prefix = lax.dynamic_slice_in_dim(prefix_len, group * req_dev, req_dev)
    live_count = jnp.sum((dest_map >= 0).astype(jnp.int32), axis=1)
    base = (member * slot_dev).astype(jnp.int32)
    rows = slot_dev * heads
    tq = min(2048, rows)
    tk = 1024
    q_flat = queries.reshape(req_dev, rows, head_dim)

    slots = req_dev * slot_dev
    capacity = (slots + devices - 1) // devices
    target = dest_map.reshape(slots)
    is_live = target >= 0
    peer = jnp.where(is_live, target // TOK_DEV, devices)
    onehot = (peer[:, None] == jnp.arange(devices, dtype=jnp.int32)[None, :]).astype(jnp.int32)
    position = jnp.sum((jnp.cumsum(onehot, axis=0) - 1) * onehot, axis=1)
    where_to = jnp.where(is_live, peer * capacity + position, devices * capacity)
    send_slots = devices * capacity
    pick = (
        where_to[None, :] == jnp.arange(send_slots, dtype=jnp.int32)[:, None]
    ).astype(jnp.bfloat16)
    row_ids = jnp.sum(
        jnp.where(
            where_to[None, :] == jnp.arange(send_slots, dtype=jnp.int32)[:, None],
            (target % TOK_DEV)[None, :] + 1,
            0,
        ),
        axis=1,
    ) - 1
    ids_in = lax.all_to_all(
        row_ids.reshape(devices, capacity),
        ("req", "tok"),
        split_axis=0,
        concat_axis=0,
        tiled=True,
    ).reshape(send_slots)
    prefix_dev = cache_kv.shape[1]
    local_kv = jnp.concatenate([cache_kv, new_kv], axis=1)
    gathered = [lax.all_gather(local_kv[0], "tok", axis=0, tiled=True)]
    gathered[0], pick, ids_in = lax.optimization_barrier((gathered[0], pick, ids_in))
    for r in range(1, req_dev):
        mine, gathered[-1] = lax.optimization_barrier((local_kv[r], gathered[-1]))
        gathered.append(lax.all_gather(mine, "tok", axis=0, tiled=True))
    outs = []
    for r in range(req_dev):
        both = gathered[r].reshape(n_member, prefix_dev + slot_dev, local_kv.shape[-1])
        scal = jnp.stack([own_prefix[r], live_count[r], base]).astype(jnp.int32)
        outs.append(
            flash_attention(q_flat, r, both, scal, heads, tq, tk, prefix_dev, slot_dev)
        )
    attended = jnp.concatenate(outs, axis=0)
    attended = attended.reshape(slots, width)
    residual_flat = residual.reshape(slots, width)
    hidden_all = (
        residual_flat.astype(jnp.float32)
        + jnp.dot(attended, w_out, preferred_element_type=jnp.float32)
        + b_out
    ).astype(jnp.bfloat16)

    send_rows = jnp.dot(pick, hidden_all, preferred_element_type=jnp.float32).astype(
        jnp.bfloat16
    )
    rows_in = lax.all_to_all(
        send_rows.reshape(devices, capacity, width),
        ("req", "tok"),
        split_axis=0,
        concat_axis=0,
        tiled=True,
    ).reshape(send_slots, width)
    land = (ids_in[None, :] == jnp.arange(TOK_DEV, dtype=jnp.int32)[:, None]).astype(
        jnp.bfloat16
    )
    hidden_state = jnp.dot(land, rows_in, preferred_element_type=jnp.float32).astype(
        jnp.bfloat16
    )
    state_f = hidden_state.astype(jnp.float32)
    mean = jnp.mean(state_f, axis=-1, keepdims=True)
    centered = state_f - mean
    variance = jnp.mean(centered * centered, axis=-1, keepdims=True)
    normed = (centered * lax.rsqrt(variance + ln_eps) * ln_gain + ln_bias).astype(jnp.bfloat16)
    units = jax.nn.gelu(
        jnp.dot(
            lax.all_gather(normed, "tok", axis=0, tiled=True),
            w_up,
            preferred_element_type=jnp.float32,
        )
        + b_up,
        approximate=True,
    )
    terms = jnp.dot(units.astype(jnp.bfloat16), w_down, preferred_element_type=jnp.float32)
    summed = lax.psum_scatter(
        terms.astype(jnp.bfloat16), "tok", scatter_dimension=0, tiled=True
    ).astype(jnp.float32)
    return (state_f + summed + b_down).astype(jnp.bfloat16)


def solution(mesh):
    in_specs = (
        P("req", "tok", None),
        P("req", "tok", None),
        P("req", "tok", None),
        P("req", "tok", None),
        P(),
        P("req", "tok"),
        P(),
        P(),
        P(),
        P(),
        P(None, "tok"),
        P("tok"),
        P("tok", None),
        P(),
    )
    out_specs = P(("req", "tok"), None)
    return jax.shard_map(
        per_device, mesh=mesh, in_specs=in_specs, out_specs=out_specs, check_vma=False
    )
```

```python
import functools
import math

import jax
import jax.numpy as jnp
from jax import lax
from jax.experimental import pallas as pl
from jax.experimental.pallas import tpu as pltpu
from jax.sharding import PartitionSpec as P

TOK_DEV = 128


neg_large = -1e30
ln_eps = 1e-05


def flash_kernel(
    scal_ref,
    q_ref,
    ck_ref,
    cv_ref,
    nk_ref,
    nv_ref,
    o_ref,
    m_sc,
    acc_sc,
    *,
    tq,
    tk,
    heads,
    head_dim,
    n_cache,
    scale,
):
    qi = pl.program_id(1)
    ki = pl.program_id(2)
    prefix = scal_ref[0]
    live = scal_ref[1]
    base = scal_ref[2]
    spt = tq // heads
    tile_lo = qi * spt
    tile_live = tile_lo < live
    q_lo = base + tile_lo
    q_hi = q_lo + spt - 1

    @pl.when(ki == 0)
    def _init():
        m_sc[...] = jnp.full(m_sc.shape, neg_large, jnp.float32)
        acc_sc[...] = jnp.zeros(acc_sc.shape, jnp.float32)

    def step(k_ref, v_ref, mask_fn):
        pieces, chunk = k_ref.shape[0], k_ref.shape[1]
        k = k_ref[...].reshape(pieces * chunk, head_dim)
        s = (
            lax.dot_general(
                k, q_ref[0], (((1,), (1,)), ((), ())), preferred_element_type=jnp.float32
            )
            * scale
        )
        mask = None
        if mask_fn is not None:
            mask = mask_fn()
            s = jnp.where(mask, s, neg_large)
        m_prev = m_sc[...]
        m_new = jnp.maximum(m_prev, jnp.max(s, axis=0, keepdims=True))
        p = jnp.exp(s - m_new)
        if mask is not None:
            p = jnp.where(mask, p, 0.0)
        alpha = jnp.exp(m_prev - m_new)
        pb = p.astype(jnp.bfloat16)
        total = alpha * acc_sc[...]
        for piece in range(pieces):
            total = total + jnp.dot(
                v_ref[piece],
                pb[piece * chunk : (piece + 1) * chunk],
                preferred_element_type=jnp.float32,
            )
        acc_sc[...] = total
        m_sc[...] = m_new

    is_cache = ki < n_cache
    kc = ki * tk
    kn = (ki - n_cache) * tk
    run_cache = is_cache & tile_live & (kc < prefix)
    full_cache = kc + tk <= prefix
    run_new = jnp.logical_not(is_cache) & tile_live & (kn <= q_hi)
    full_new = kn + tk - 1 <= q_lo

    def cache_mask():
        key = lax.broadcasted_iota(jnp.int32, (tk, tq), 0) + kc
        return key < prefix

    def new_mask():
        key = lax.broadcasted_iota(jnp.int32, (tk, tq), 0) + kn
        slot = lax.broadcasted_iota(jnp.int32, (tk, tq), 1) // heads + q_lo
        return key <= slot

    @pl.when(run_cache & full_cache)
    def _c_full():
        step(ck_ref, cv_ref, None)

    @pl.when(run_cache & jnp.logical_not(full_cache))
    def _c_part():
        step(ck_ref, cv_ref, cache_mask)

    @pl.when(run_new & full_new)
    def _n_full():
        step(nk_ref, nv_ref, None)

    @pl.when(run_new & jnp.logical_not(full_new))
    def _n_part():
        step(nk_ref, nv_ref, new_mask)

    @pl.when(ki == pl.num_programs(2) - 1)
    def _fin():
        acc = acc_sc[...]
        l = acc[head_dim : head_dim + 1]
        safe = jnp.where(l > 0, l, 1.0)
        out = jnp.where(l > 0, acc[:head_dim] / safe, 0.0)
        o_ref[0] = jnp.transpose(out).astype(o_ref.dtype)


def flash_attention(q, req, gc, gn, scal, heads, tq, tk):
    n_req, rows, head_dim = q.shape
    n_member, prefix_dev = gc.shape[0], gc.shape[1]
    slot_dev = gn.shape[1]
    n_cache = n_member * prefix_dev // tk
    n_new = n_member * slot_dev // tk
    per_cache = tk // prefix_dev
    per_new = tk // slot_dev
    spt = tq // heads
    scale = 1.0 / math.sqrt(head_dim)
    vc = jnp.concatenate(
        [jnp.swapaxes(gc[:, :, head_dim:], 1, 2), jnp.ones((n_member, 8, prefix_dev), gc.dtype)],
        axis=1,
    )
    vn = jnp.concatenate(
        [jnp.swapaxes(gn[:, :, head_dim:], 1, 2), jnp.ones((n_member, 8, slot_dev), gn.dtype)],
        axis=1,
    )
    ext = head_dim + 8

    def q_map(r, qi, ki, s):
        return (req, qi, 0)

    def o_map(r, qi, ki, s):
        return (0, qi, 0)

    def c_block(ki, s):
        last = jnp.maximum((s[0] + tk - 1) // tk - 1, 0)
        return jnp.minimum(ki, last)

    def n_block(qi, ki, s):
        q_hi = s[2] + (qi + 1) * spt - 1
        last = jnp.minimum(q_hi // tk, n_new - 1)
        return jnp.clip(ki - n_cache, 0, last)

    kernel = functools.partial(
        flash_kernel,
        tq=tq,
        tk=tk,
        heads=heads,
        head_dim=head_dim,
        n_cache=n_cache,
        scale=scale,
    )
    grid_spec = pltpu.PrefetchScalarGridSpec(
        num_scalar_prefetch=1,
        grid=(1, rows // tq, n_cache + n_new),
        in_specs=[
            pl.BlockSpec((1, tq, head_dim), q_map),
            pl.BlockSpec(
                (per_cache, prefix_dev, head_dim),
                lambda r, qi, ki, s: (c_block(ki, s), 0, 0),
            ),
            pl.BlockSpec(
                (per_cache, ext, prefix_dev),
                lambda r, qi, ki, s: (c_block(ki, s), 0, 0),
            ),
            pl.BlockSpec(
                (per_new, slot_dev, head_dim),
                lambda r, qi, ki, s: (n_block(qi, ki, s), 0, 0),
            ),
            pl.BlockSpec(
                (per_new, ext, slot_dev),
                lambda r, qi, ki, s: (n_block(qi, ki, s), 0, 0),
            ),
        ],
        out_specs=pl.BlockSpec((1, tq, head_dim), o_map),
        scratch_shapes=[
            pltpu.VMEM((1, tq), jnp.float32),
            pltpu.VMEM((ext, tq), jnp.float32),
        ],
    )
    return pl.pallas_call(
        kernel,
        grid_spec=grid_spec,
        out_shape=jax.ShapeDtypeStruct((1, rows, head_dim), jnp.bfloat16),
    )(scal, q, gc, vc, gn, vn)


def per_device(
    queries,
    new_kv,
    cache_kv,
    residual,
    prefix_len,
    dest_map,
    w_out,
    b_out,
    ln_gain,
    ln_bias,
    w_up,
    b_up,
    w_down,
    b_down,
):
    group = lax.axis_index("req")
    member = lax.axis_index("tok")
    n_group = lax.axis_size("req")
    n_member = lax.axis_size("tok")
    devices = n_group * n_member
    req_dev, slot_dev, width = queries.shape
    head_dim = new_kv.shape[2] // 2
    heads = width // head_dim
    own_prefix = lax.dynamic_slice_in_dim(prefix_len, group * req_dev, req_dev)
    live_count = jnp.sum((dest_map >= 0).astype(jnp.int32), axis=1)
    base = (member * slot_dev).astype(jnp.int32)
    rows = slot_dev * heads
    tq = min(2048, rows)
    tk = 1024
    q_flat = queries.reshape(req_dev, rows, head_dim)

    slots = req_dev * slot_dev
    capacity = (slots + devices - 1) // devices
    target = dest_map.reshape(slots)
    is_live = target >= 0
    peer = jnp.where(is_live, target // TOK_DEV, devices)
    onehot = (peer[:, None] == jnp.arange(devices, dtype=jnp.int32)[None, :]).astype(jnp.int32)
    position = jnp.sum((jnp.cumsum(onehot, axis=0) - 1) * onehot, axis=1)
    where_to = jnp.where(is_live, peer * capacity + position, devices * capacity)
    send_slots = devices * capacity
    pick = (
        where_to[None, :] == jnp.arange(send_slots, dtype=jnp.int32)[:, None]
    ).astype(jnp.bfloat16)
    row_ids = jnp.sum(
        jnp.where(
            where_to[None, :] == jnp.arange(send_slots, dtype=jnp.int32)[:, None],
            (target % TOK_DEV)[None, :] + 1,
            0,
        ),
        axis=1,
    ) - 1
    ids_in = lax.all_to_all(
        row_ids.reshape(devices, capacity),
        ("req", "tok"),
        split_axis=0,
        concat_axis=0,
        tiled=True,
    ).reshape(send_slots)
    def exchange(cache_r, new_r):
        cache_in = [cache_r]
        new_in = [new_r]
        for step in range(n_member - 1, 0, -1):
            cache_in.append(
                lax.ppermute(
                    cache_r, "tok", [(i, (i + step) % n_member) for i in range(n_member)]
                )
            )
            new_in.append(
                lax.ppermute(new_r, "tok", [(i, i + step) for i in range(n_member - step)])
            )
        return (
            jnp.roll(jnp.stack(cache_in), member, axis=0),
            jnp.roll(jnp.stack(new_in), member, axis=0),
        )

    gathered = [exchange(cache_kv[0], new_kv[0])]
    gathered[0], pick, ids_in = lax.optimization_barrier((gathered[0], pick, ids_in))
    for r in range(1, req_dev):
        mine, gathered[-1] = lax.optimization_barrier(((cache_kv[r], new_kv[r]), gathered[-1]))
        gathered.append(exchange(*mine))
    outs = []
    for r in range(req_dev):
        gc, gn = gathered[r]
        scal = jnp.stack([own_prefix[r], live_count[r], base]).astype(jnp.int32)
        outs.append(flash_attention(q_flat, r, gc, gn, scal, heads, tq, tk))
    attended = jnp.concatenate(outs, axis=0)
    attended = attended.reshape(slots, width)
    residual_flat = residual.reshape(slots, width)
    hidden_all = (
        residual_flat.astype(jnp.float32)
        + jnp.dot(attended, w_out, preferred_element_type=jnp.float32)
        + b_out
    ).astype(jnp.bfloat16)

    send_rows = jnp.dot(pick, hidden_all, preferred_element_type=jnp.float32).astype(
        jnp.bfloat16
    )
    rows_in = lax.all_to_all(
        send_rows.reshape(devices, capacity, width),
        ("req", "tok"),
        split_axis=0,
        concat_axis=0,
        tiled=True,
    ).reshape(send_slots, width)
    land = (ids_in[None, :] == jnp.arange(TOK_DEV, dtype=jnp.int32)[:, None]).astype(
        jnp.bfloat16
    )
    hidden_state = jnp.dot(land, rows_in, preferred_element_type=jnp.float32).astype(
        jnp.bfloat16
    )
    state_f = hidden_state.astype(jnp.float32)
    mean = jnp.mean(state_f, axis=-1, keepdims=True)
    centered = state_f - mean
    variance = jnp.mean(centered * centered, axis=-1, keepdims=True)
    normed = (centered * lax.rsqrt(variance + ln_eps) * ln_gain + ln_bias).astype(jnp.bfloat16)
    units = jax.nn.gelu(
        jnp.dot(
            lax.all_gather(normed, "tok", axis=0, tiled=True),
            w_up,
            preferred_element_type=jnp.float32,
        )
        + b_up,
        approximate=True,
    )
    terms = jnp.dot(units.astype(jnp.bfloat16), w_down, preferred_element_type=jnp.float32)
    summed = lax.psum_scatter(
        terms.astype(jnp.bfloat16), "tok", scatter_dimension=0, tiled=True
    ).astype(jnp.float32)
    return (state_f + summed + b_down).astype(jnp.bfloat16)


def solution(mesh):
    in_specs = (
        P("req", "tok", None),
        P("req", "tok", None),
        P("req", "tok", None),
        P("req", "tok", None),
        P(),
        P("req", "tok"),
        P(),
        P(),
        P(),
        P(),
        P(None, "tok"),
        P("tok"),
        P("tok", None),
        P(),
    )
    out_specs = P(("req", "tok"), None)
    return jax.shard_map(
        per_device, mesh=mesh, in_specs=in_specs, out_specs=out_specs, check_vma=False
    )
```

```python
import functools
import math

import jax
import jax.numpy as jnp
from jax import lax
from jax.experimental import pallas as pl
from jax.experimental.pallas import tpu as pltpu
from jax.sharding import PartitionSpec as P

TOK_DEV = 128


neg_large = -1e30
ln_eps = 1e-05


def flash_kernel(
    scal_ref,
    q_ref,
    ck_ref,
    cv_ref,
    nk_ref,
    nv_ref,
    o_ref,
    m_sc,
    acc_sc,
    *,
    tq,
    tk,
    heads,
    head_dim,
    n_cache,
    scale,
):
    qi = pl.program_id(1)
    ki = pl.program_id(2)
    prefix = scal_ref[0]
    live = scal_ref[1]
    base = scal_ref[2]
    spt = tq // heads
    tile_lo = qi * spt
    tile_live = tile_lo < live
    q_lo = base + tile_lo
    q_hi = q_lo + spt - 1

    @pl.when(ki == 0)
    def _init():
        m_sc[...] = jnp.full(m_sc.shape, neg_large, jnp.float32)
        acc_sc[...] = jnp.zeros(acc_sc.shape, jnp.float32)

    def step(k_ref, v_ref, mask_fn):
        pieces, chunk = k_ref.shape[0], k_ref.shape[1]
        k = k_ref[...].reshape(pieces * chunk, head_dim)
        s = (
            lax.dot_general(
                k, q_ref[0], (((1,), (1,)), ((), ())), preferred_element_type=jnp.float32
            )
            * scale
        )
        mask = None
        if mask_fn is not None:
            mask = mask_fn()
            s = jnp.where(mask, s, neg_large)
        m_prev = m_sc[...]
        m_new = jnp.maximum(m_prev, jnp.max(s, axis=0, keepdims=True))
        p = jnp.exp(s - m_new)
        if mask is not None:
            p = jnp.where(mask, p, 0.0)
        alpha = jnp.exp(m_prev - m_new)
        pb = p.astype(jnp.bfloat16)
        total = alpha * acc_sc[...]
        for piece in range(pieces):
            total = total + jnp.dot(
                v_ref[piece],
                pb[piece * chunk : (piece + 1) * chunk],
                preferred_element_type=jnp.float32,
            )
        acc_sc[...] = total
        m_sc[...] = m_new

    is_cache = ki < n_cache
    kc = ki * tk
    kn = (ki - n_cache) * tk
    run_cache = is_cache & tile_live & (kc < prefix)
    full_cache = kc + tk <= prefix
    run_new = jnp.logical_not(is_cache) & tile_live & (kn <= q_hi)
    full_new = kn + tk - 1 <= q_lo

    def cache_mask():
        key = lax.broadcasted_iota(jnp.int32, (tk, tq), 0) + kc
        return key < prefix

    def new_mask():
        key = lax.broadcasted_iota(jnp.int32, (tk, tq), 0) + kn
        slot = lax.broadcasted_iota(jnp.int32, (tk, tq), 1) // heads + q_lo
        return key <= slot

    @pl.when(run_cache & full_cache)
    def _c_full():
        step(ck_ref, cv_ref, None)

    @pl.when(run_cache & jnp.logical_not(full_cache))
    def _c_part():
        step(ck_ref, cv_ref, cache_mask)

    @pl.when(run_new & full_new)
    def _n_full():
        step(nk_ref, nv_ref, None)

    @pl.when(run_new & jnp.logical_not(full_new))
    def _n_part():
        step(nk_ref, nv_ref, new_mask)

    @pl.when(ki == pl.num_programs(2) - 1)
    def _fin():
        acc = acc_sc[...]
        l = acc[head_dim : head_dim + 1]
        safe = jnp.where(l > 0, l, 1.0)
        out = jnp.where(l > 0, acc[:head_dim] / safe, 0.0)
        o_ref[0] = jnp.transpose(out).astype(o_ref.dtype)


def flash_attention(q, req, both, scal, heads, tq, tk, prefix_dev, slot_dev):
    n_req, rows, head_dim = q.shape
    n_member = both.shape[0]
    n_cache = n_member * prefix_dev // tk
    n_new = n_member * slot_dev // tk
    per_cache = tk // prefix_dev
    per_new = tk // slot_dev
    new_at = prefix_dev // slot_dev
    spt = tq // heads
    scale = 1.0 / math.sqrt(head_dim)
    ones = jnp.ones((n_member, 8, both.shape[1]), jnp.bfloat16)
    vt = jnp.concatenate([jnp.swapaxes(both[:, :, head_dim:], 1, 2), ones], axis=1)
    ext = head_dim + 8

    def q_map(r, qi, ki, s):
        return (req, qi, 0)

    def o_map(r, qi, ki, s):
        return (0, qi, 0)

    def c_block(ki, s):
        last = jnp.maximum((s[0] + tk - 1) // tk - 1, 0)
        return jnp.minimum(ki, last)

    def n_block(qi, ki, s):
        q_hi = s[2] + (qi + 1) * spt - 1
        last = jnp.minimum(q_hi // tk, n_new - 1)
        return jnp.clip(ki - n_cache, 0, last)

    kernel = functools.partial(
        flash_kernel,
        tq=tq,
        tk=tk,
        heads=heads,
        head_dim=head_dim,
        n_cache=n_cache,
        scale=scale,
    )
    grid_spec = pltpu.PrefetchScalarGridSpec(
        num_scalar_prefetch=1,
        grid=(1, rows // tq, n_cache + n_new),
        in_specs=[
            pl.BlockSpec((1, tq, head_dim), q_map),
            pl.BlockSpec(
                (per_cache, prefix_dev, head_dim),
                lambda r, qi, ki, s: (c_block(ki, s), 0, 0),
            ),
            pl.BlockSpec(
                (per_cache, ext, prefix_dev),
                lambda r, qi, ki, s: (c_block(ki, s), 0, 0),
            ),
            pl.BlockSpec(
                (per_new, slot_dev, head_dim),
                lambda r, qi, ki, s: (n_block(qi, ki, s), new_at, 0),
            ),
            pl.BlockSpec(
                (per_new, ext, slot_dev),
                lambda r, qi, ki, s: (n_block(qi, ki, s), 0, new_at),
            ),
        ],
        out_specs=pl.BlockSpec((1, tq, head_dim), o_map),
        scratch_shapes=[
            pltpu.VMEM((1, tq), jnp.float32),
            pltpu.VMEM((ext, tq), jnp.float32),
        ],
    )
    return pl.pallas_call(
        kernel,
        grid_spec=grid_spec,
        out_shape=jax.ShapeDtypeStruct((1, rows, head_dim), jnp.bfloat16),
    )(scal, q, both, vt, both, vt)


def per_device(
    queries,
    new_kv,
    cache_kv,
    residual,
    prefix_len,
    dest_map,
    w_out,
    b_out,
    ln_gain,
    ln_bias,
    w_up,
    b_up,
    w_down,
    b_down,
):
    group = lax.axis_index("req")
    member = lax.axis_index("tok")
    n_group = lax.axis_size("req")
    n_member = lax.axis_size("tok")
    devices = n_group * n_member
    req_dev, slot_dev, width = queries.shape
    head_dim = new_kv.shape[2] // 2
    heads = width // head_dim
    own_prefix = lax.dynamic_slice_in_dim(prefix_len, group * req_dev, req_dev)
    live_count = jnp.sum((dest_map >= 0).astype(jnp.int32), axis=1)
    base = (member * slot_dev).astype(jnp.int32)
    rows = slot_dev * heads
    tq = min(2048, rows)
    tk = 1024
    q_flat = queries.reshape(req_dev, rows, head_dim)

    slots = req_dev * slot_dev
    capacity = (slots + devices - 1) // devices
    target = dest_map.reshape(slots)
    is_live = target >= 0
    peer = jnp.where(is_live, target // TOK_DEV, devices)
    onehot = (peer[:, None] == jnp.arange(devices, dtype=jnp.int32)[None, :]).astype(jnp.int32)
    position = jnp.sum((jnp.cumsum(onehot, axis=0) - 1) * onehot, axis=1)
    where_to = jnp.where(is_live, peer * capacity + position, devices * capacity)
    send_slots = devices * capacity
    pick = (
        where_to[None, :] == jnp.arange(send_slots, dtype=jnp.int32)[:, None]
    ).astype(jnp.bfloat16)
    row_ids = jnp.sum(
        jnp.where(
            where_to[None, :] == jnp.arange(send_slots, dtype=jnp.int32)[:, None],
            (target % TOK_DEV)[None, :] + 1,
            0,
        ),
        axis=1,
    ) - 1
    ids_in = lax.all_to_all(
        row_ids.reshape(devices, capacity),
        ("req", "tok"),
        split_axis=0,
        concat_axis=0,
        tiled=True,
    ).reshape(send_slots)
    prefix_dev = cache_kv.shape[1]
    local_kv = jnp.concatenate([cache_kv, new_kv], axis=1)
    gathered = [lax.all_gather(local_kv[0], "tok", axis=0, tiled=True)]
    gathered[0], pick, ids_in = lax.optimization_barrier((gathered[0], pick, ids_in))
    for r in range(1, req_dev):
        mine, gathered[-1] = lax.optimization_barrier((local_kv[r], gathered[-1]))
        gathered.append(lax.all_gather(mine, "tok", axis=0, tiled=True))
    outs = []
    for r in range(req_dev):
        both = gathered[r].reshape(n_member, prefix_dev + slot_dev, local_kv.shape[-1])
        scal = jnp.stack([own_prefix[r], live_count[r], base]).astype(jnp.int32)
        attended = flash_attention(
            q_flat, r, both, scal, heads, tq, tk, prefix_dev, slot_dev
        ).reshape(slot_dev, width)
        hidden_r = (
            residual[r].astype(jnp.float32)
            + jnp.dot(attended, w_out, preferred_element_type=jnp.float32)
            + b_out
        ).astype(jnp.bfloat16)
        outs.append(
            jnp.dot(
                pick[:, r * slot_dev : (r + 1) * slot_dev],
                hidden_r,
                preferred_element_type=jnp.float32,
            )
        )
    send_rows = functools.reduce(jnp.add, outs).astype(jnp.bfloat16)
    rows_in = lax.all_to_all(
        send_rows.reshape(devices, capacity, width),
        ("req", "tok"),
        split_axis=0,
        concat_axis=0,
        tiled=True,
    ).reshape(send_slots, width)
    land = (ids_in[None, :] == jnp.arange(TOK_DEV, dtype=jnp.int32)[:, None]).astype(
        jnp.bfloat16
    )
    hidden_state = jnp.dot(land, rows_in, preferred_element_type=jnp.float32).astype(
        jnp.bfloat16
    )
    state_f = hidden_state.astype(jnp.float32)
    mean = jnp.mean(state_f, axis=-1, keepdims=True)
    centered = state_f - mean
    variance = jnp.mean(centered * centered, axis=-1, keepdims=True)
    normed = (centered * lax.rsqrt(variance + ln_eps) * ln_gain + ln_bias).astype(jnp.bfloat16)
    units = jax.nn.gelu(
        jnp.dot(
            lax.all_gather(normed, "tok", axis=0, tiled=True),
            w_up,
            preferred_element_type=jnp.float32,
        )
        + b_up,
        approximate=True,
    )
    terms = jnp.dot(units.astype(jnp.bfloat16), w_down, preferred_element_type=jnp.float32)
    summed = lax.psum_scatter(
        terms.astype(jnp.bfloat16), "tok", scatter_dimension=0, tiled=True
    ).astype(jnp.float32)
    return (state_f + summed + b_down).astype(jnp.bfloat16)


def solution(mesh):
    in_specs = (
        P("req", "tok", None),
        P("req", "tok", None),
        P("req", "tok", None),
        P("req", "tok", None),
        P(),
        P("req", "tok"),
        P(),
        P(),
        P(),
        P(),
        P(None, "tok"),
        P("tok"),
        P("tok", None),
        P(),
    )
    out_specs = P(("req", "tok"), None)
    return jax.shard_map(
        per_device, mesh=mesh, in_specs=in_specs, out_specs=out_specs, check_vma=False
    )
```

```python
import functools
import math

import jax
import jax.numpy as jnp
from jax import lax
from jax.experimental import pallas as pl
from jax.experimental.pallas import tpu as pltpu
from jax.sharding import PartitionSpec as P

TOK_DEV = 128


neg_large = -1e30
ln_eps = 1e-05


def flash_kernel(
    scal_ref,
    q_ref,
    ck_ref,
    cv_ref,
    nk_ref,
    nv_ref,
    o_ref,
    m_sc,
    acc_sc,
    *,
    tq,
    tk,
    heads,
    head_dim,
    n_cache,
    n_req,
    scale,
):
    r = pl.program_id(0)
    qi = pl.program_id(1)
    ki = pl.program_id(2)
    prefix = scal_ref[r]
    live = scal_ref[n_req + r]
    base = scal_ref[2 * n_req]
    spt = tq // heads
    tile_lo = qi * spt
    tile_live = tile_lo < live
    q_lo = base + tile_lo
    q_hi = q_lo + spt - 1

    @pl.when(ki == 0)
    def _init():
        m_sc[...] = jnp.full(m_sc.shape, neg_large, jnp.float32)
        acc_sc[...] = jnp.zeros(acc_sc.shape, jnp.float32)

    def step(k_ref, v_ref, mask_fn):
        pieces, chunk = k_ref.shape[1], k_ref.shape[2]
        k = k_ref[0].reshape(pieces * chunk, head_dim)
        s = (
            lax.dot_general(
                k, q_ref[0], (((1,), (1,)), ((), ())), preferred_element_type=jnp.float32
            )
            * scale
        )
        mask = None
        if mask_fn is not None:
            mask = mask_fn()
            s = jnp.where(mask, s, neg_large)
        m_prev = m_sc[...]
        m_new = jnp.maximum(m_prev, jnp.max(s, axis=0, keepdims=True))
        p = jnp.exp(s - m_new)
        if mask is not None:
            p = jnp.where(mask, p, 0.0)
        alpha = jnp.exp(m_prev - m_new)
        pb = p.astype(jnp.bfloat16)
        total = alpha * acc_sc[...]
        for piece in range(pieces):
            total = total + jnp.dot(
                v_ref[0, piece],
                pb[piece * chunk : (piece + 1) * chunk],
                preferred_element_type=jnp.float32,
            )
        acc_sc[...] = total
        m_sc[...] = m_new

    is_cache = ki < n_cache
    kc = ki * tk
    kn = (ki - n_cache) * tk
    run_cache = is_cache & tile_live & (kc < prefix)
    full_cache = kc + tk <= prefix
    run_new = jnp.logical_not(is_cache) & tile_live & (kn <= q_hi)
    full_new = kn + tk - 1 <= q_lo

    def cache_mask():
        key = lax.broadcasted_iota(jnp.int32, (tk, tq), 0) + kc
        return key < prefix

    def new_mask():
        key = lax.broadcasted_iota(jnp.int32, (tk, tq), 0) + kn
        slot = lax.broadcasted_iota(jnp.int32, (tk, tq), 1) // heads + q_lo
        return key <= slot

    @pl.when(run_cache & full_cache)
    def _c_full():
        step(ck_ref, cv_ref, None)

    @pl.when(run_cache & jnp.logical_not(full_cache))
    def _c_part():
        step(ck_ref, cv_ref, cache_mask)

    @pl.when(run_new & full_new)
    def _n_full():
        step(nk_ref, nv_ref, None)

    @pl.when(run_new & jnp.logical_not(full_new))
    def _n_part():
        step(nk_ref, nv_ref, new_mask)

    @pl.when(ki == pl.num_programs(2) - 1)
    def _fin():
        acc = acc_sc[...]
        l = acc[head_dim : head_dim + 1]
        safe = jnp.where(l > 0, l, 1.0)
        out = jnp.where(l > 0, acc[:head_dim] / safe, 0.0)
        o_ref[0] = jnp.transpose(out).astype(o_ref.dtype)


def flash_attention(q, both, scal, heads, tq, tk, prefix_dev, slot_dev):
    n_req, rows, head_dim = q.shape
    n_member = both.shape[1]
    n_cache = n_member * prefix_dev // tk
    n_new = n_member * slot_dev // tk
    per_cache = tk // prefix_dev
    per_new = tk // slot_dev
    new_at = prefix_dev // slot_dev
    spt = tq // heads
    scale = 1.0 / math.sqrt(head_dim)
    ones = jnp.ones((n_req, n_member, 8, both.shape[2]), jnp.bfloat16)
    vt = jnp.concatenate([jnp.swapaxes(both[..., head_dim:], 2, 3), ones], axis=2)
    ext = head_dim + 8

    def q_map(r, qi, ki, s):
        return (r, qi, 0)

    def c_block(r, ki, s):
        last = jnp.maximum((s[r] + tk - 1) // tk - 1, 0)
        return jnp.minimum(ki, last)

    def n_block(r, qi, ki, s):
        q_hi = s[2 * n_req] + (qi + 1) * spt - 1
        last = jnp.minimum(q_hi // tk, n_new - 1)
        return jnp.clip(ki - n_cache, 0, last)

    kernel = functools.partial(
        flash_kernel,
        tq=tq,
        tk=tk,
        heads=heads,
        head_dim=head_dim,
        n_cache=n_cache,
        n_req=n_req,
        scale=scale,
    )
    grid_spec = pltpu.PrefetchScalarGridSpec(
        num_scalar_prefetch=1,
        grid=(n_req, rows // tq, n_cache + n_new),
        in_specs=[
            pl.BlockSpec((1, tq, head_dim), q_map),
            pl.BlockSpec(
                (1, per_cache, prefix_dev, head_dim),
                lambda r, qi, ki, s: (r, c_block(r, ki, s), 0, 0),
            ),
            pl.BlockSpec(
                (1, per_cache, ext, prefix_dev),
                lambda r, qi, ki, s: (r, c_block(r, ki, s), 0, 0),
            ),
            pl.BlockSpec(
                (1, per_new, slot_dev, head_dim),
                lambda r, qi, ki, s: (r, n_block(r, qi, ki, s), new_at, 0),
            ),
            pl.BlockSpec(
                (1, per_new, ext, slot_dev),
                lambda r, qi, ki, s: (r, n_block(r, qi, ki, s), 0, new_at),
            ),
        ],
        out_specs=pl.BlockSpec((1, tq, head_dim), q_map),
        scratch_shapes=[
            pltpu.VMEM((1, tq), jnp.float32),
            pltpu.VMEM((ext, tq), jnp.float32),
        ],
    )
    return pl.pallas_call(
        kernel,
        grid_spec=grid_spec,
        out_shape=jax.ShapeDtypeStruct((n_req, rows, head_dim), jnp.bfloat16),
    )(scal, q, both, vt, both, vt)


def per_device(
    queries,
    new_kv,
    cache_kv,
    residual,
    prefix_len,
    dest_map,
    w_out,
    b_out,
    ln_gain,
    ln_bias,
    w_up,
    b_up,
    w_down,
    b_down,
):
    group = lax.axis_index("req")
    member = lax.axis_index("tok")
    n_group = lax.axis_size("req")
    n_member = lax.axis_size("tok")
    devices = n_group * n_member
    req_dev, slot_dev, width = queries.shape
    head_dim = new_kv.shape[2] // 2
    heads = width // head_dim
    own_prefix = lax.dynamic_slice_in_dim(prefix_len, group * req_dev, req_dev)
    live_count = jnp.sum((dest_map >= 0).astype(jnp.int32), axis=1)
    base = (member * slot_dev).astype(jnp.int32)
    rows = slot_dev * heads
    tq = min(2048, rows)
    tk = 1024
    q_flat = queries.reshape(req_dev, rows, head_dim)

    slots = req_dev * slot_dev
    capacity = (slots + devices - 1) // devices
    target = dest_map.reshape(slots)
    is_live = target >= 0
    peer = jnp.where(is_live, target // TOK_DEV, devices)
    onehot = (peer[:, None] == jnp.arange(devices, dtype=jnp.int32)[None, :]).astype(jnp.int32)
    position = jnp.sum((jnp.cumsum(onehot, axis=0) - 1) * onehot, axis=1)
    where_to = jnp.where(is_live, peer * capacity + position, devices * capacity)
    send_slots = devices * capacity
    pick = (
        where_to[None, :] == jnp.arange(send_slots, dtype=jnp.int32)[:, None]
    ).astype(jnp.bfloat16)
    row_ids = jnp.sum(
        jnp.where(
            where_to[None, :] == jnp.arange(send_slots, dtype=jnp.int32)[:, None],
            (target % TOK_DEV)[None, :] + 1,
            0,
        ),
        axis=1,
    ) - 1
    ids_in = lax.all_to_all(
        row_ids.reshape(devices, capacity),
        ("req", "tok"),
        split_axis=0,
        concat_axis=0,
        tiled=True,
    ).reshape(send_slots)
    prefix_dev = cache_kv.shape[1]
    local_kv = jnp.concatenate([cache_kv, new_kv], axis=1)
    gathered = lax.all_gather(local_kv, "tok", axis=1, tiled=True)
    gathered, pick, ids_in = lax.optimization_barrier((gathered, pick, ids_in))
    both = gathered.reshape(req_dev, n_member, prefix_dev + slot_dev, local_kv.shape[-1])
    scal = jnp.concatenate([own_prefix, live_count, base[None]]).astype(jnp.int32)
    attended = flash_attention(q_flat, both, scal, heads, tq, tk, prefix_dev, slot_dev)
    attended = attended.reshape(slots, width)
    hidden_all = (
        residual.reshape(slots, width).astype(jnp.float32)
        + jnp.dot(attended, w_out, preferred_element_type=jnp.float32)
        + b_out
    ).astype(jnp.bfloat16)
    send_rows = jnp.dot(pick, hidden_all, preferred_element_type=jnp.float32).astype(
        jnp.bfloat16
    )
    rows_in = lax.all_to_all(
        send_rows.reshape(devices, capacity, width),
        ("req", "tok"),
        split_axis=0,
        concat_axis=0,
        tiled=True,
    ).reshape(send_slots, width)
    land = (ids_in[None, :] == jnp.arange(TOK_DEV, dtype=jnp.int32)[:, None]).astype(
        jnp.bfloat16
    )
    hidden_state = jnp.dot(land, rows_in, preferred_element_type=jnp.float32).astype(
        jnp.bfloat16
    )
    state_f = hidden_state.astype(jnp.float32)
    mean = jnp.mean(state_f, axis=-1, keepdims=True)
    centered = state_f - mean
    variance = jnp.mean(centered * centered, axis=-1, keepdims=True)
    normed = (centered * lax.rsqrt(variance + ln_eps) * ln_gain + ln_bias).astype(jnp.bfloat16)
    units = jax.nn.gelu(
        jnp.dot(
            lax.all_gather(normed, "tok", axis=0, tiled=True),
            w_up,
            preferred_element_type=jnp.float32,
        )
        + b_up,
        approximate=True,
    )
    terms = jnp.dot(units.astype(jnp.bfloat16), w_down, preferred_element_type=jnp.float32)
    summed = lax.psum_scatter(
        terms.astype(jnp.bfloat16), "tok", scatter_dimension=0, tiled=True
    ).astype(jnp.float32)
    return (state_f + summed + b_down).astype(jnp.bfloat16)


def solution(mesh):
    in_specs = (
        P("req", "tok", None),
        P("req", "tok", None),
        P("req", "tok", None),
        P("req", "tok", None),
        P(),
        P("req", "tok"),
        P(),
        P(),
        P(),
        P(),
        P(None, "tok"),
        P("tok"),
        P("tok", None),
        P(),
    )
    out_specs = P(("req", "tok"), None)
    return jax.shard_map(
        per_device, mesh=mesh, in_specs=in_specs, out_specs=out_specs, check_vma=False
    )
```

```python
import functools
import math

import jax
import jax.numpy as jnp
from jax import lax
from jax.experimental import pallas as pl
from jax.experimental.pallas import tpu as pltpu
from jax.sharding import PartitionSpec as P

TOK_DEV = 128


neg_large = -1e30
ln_eps = 1e-05


def flash_kernel(
    scal_ref,
    q_ref,
    ck_ref,
    cv_ref,
    nk_ref,
    nv_ref,
    o_ref,
    m_sc,
    acc_sc,
    *,
    tq,
    tk,
    heads,
    head_dim,
    n_cache,
    scale,
):
    qi = pl.program_id(1)
    ki = pl.program_id(2)
    prefix = scal_ref[0]
    live = scal_ref[1]
    base = scal_ref[2]
    spt = tq // heads
    tile_lo = qi * spt
    tile_live = tile_lo < live
    q_lo = base + tile_lo
    q_hi = q_lo + spt - 1

    @pl.when(ki == 0)
    def _init():
        m_sc[...] = jnp.full(m_sc.shape, neg_large, jnp.float32)
        acc_sc[...] = jnp.zeros(acc_sc.shape, jnp.float32)

    def step(k_ref, v_ref, mask_fn):
        pieces, chunk = k_ref.shape[0], k_ref.shape[1]
        k = k_ref[...].reshape(pieces * chunk, head_dim)
        s = (
            lax.dot_general(
                k, q_ref[0], (((1,), (1,)), ((), ())), preferred_element_type=jnp.float32
            )
            * scale
        )
        mask = None
        if mask_fn is not None:
            mask = mask_fn()
            s = jnp.where(mask, s, neg_large)
        m_prev = m_sc[...]
        m_new = jnp.maximum(m_prev, jnp.max(s, axis=0, keepdims=True))
        p = jnp.exp(s - m_new)
        if mask is not None:
            p = jnp.where(mask, p, 0.0)
        alpha = jnp.exp(m_prev - m_new)
        pb = p.astype(jnp.bfloat16)
        total = alpha * acc_sc[...]
        for piece in range(pieces):
            total = total + jnp.dot(
                v_ref[piece],
                pb[piece * chunk : (piece + 1) * chunk],
                preferred_element_type=jnp.float32,
            )
        acc_sc[...] = total
        m_sc[...] = m_new

    is_cache = ki < n_cache
    kc = ki * tk
    kn = (ki - n_cache) * tk
    run_cache = is_cache & tile_live & (kc < prefix)
    full_cache = kc + tk <= prefix
    run_new = jnp.logical_not(is_cache) & tile_live & (kn <= q_hi)
    full_new = kn + tk - 1 <= q_lo

    def cache_mask():
        key = lax.broadcasted_iota(jnp.int32, (tk, tq), 0) + kc
        return key < prefix

    def new_mask():
        key = lax.broadcasted_iota(jnp.int32, (tk, tq), 0) + kn
        slot = lax.broadcasted_iota(jnp.int32, (tk, tq), 1) // heads + q_lo
        return key <= slot

    @pl.when(run_cache & full_cache)
    def _c_full():
        step(ck_ref, cv_ref, None)

    @pl.when(run_cache & jnp.logical_not(full_cache))
    def _c_part():
        step(ck_ref, cv_ref, cache_mask)

    @pl.when(run_new & full_new)
    def _n_full():
        step(nk_ref, nv_ref, None)

    @pl.when(run_new & jnp.logical_not(full_new))
    def _n_part():
        step(nk_ref, nv_ref, new_mask)

    @pl.when(ki == pl.num_programs(2) - 1)
    def _fin():
        acc = acc_sc[...]
        l = acc[head_dim : head_dim + 1]
        safe = jnp.where(l > 0, l, 1.0)
        out = jnp.where(l > 0, acc[:head_dim] / safe, 0.0)
        o_ref[0] = jnp.transpose(out).astype(o_ref.dtype)


def flash_attention(q, both, scal, heads, tq, tk, prefix_dev, slot_dev):
    n_req, rows, head_dim = q.shape
    n_member = both.shape[0]
    n_cache = n_member * prefix_dev // tk
    n_new = n_member * slot_dev // tk
    per_cache = tk // prefix_dev
    per_new = tk // slot_dev
    new_at = prefix_dev // slot_dev
    spt = tq // heads
    scale = 1.0 / math.sqrt(head_dim)
    ones = jnp.ones((n_member, 8, both.shape[1]), jnp.bfloat16)
    vt = jnp.concatenate([jnp.swapaxes(both[:, :, head_dim:], 1, 2), ones], axis=1)
    ext = head_dim + 8

    def q_map(r, qi, ki, s):
        return (s[3], qi, 0)

    def o_map(r, qi, ki, s):
        return (0, qi, 0)

    def c_block(ki, s):
        last = jnp.maximum((s[0] + tk - 1) // tk - 1, 0)
        return jnp.minimum(ki, last)

    def n_block(qi, ki, s):
        q_hi = s[2] + (qi + 1) * spt - 1
        last = jnp.minimum(q_hi // tk, n_new - 1)
        return jnp.clip(ki - n_cache, 0, last)

    kernel = functools.partial(
        flash_kernel,
        tq=tq,
        tk=tk,
        heads=heads,
        head_dim=head_dim,
        n_cache=n_cache,
        scale=scale,
    )
    grid_spec = pltpu.PrefetchScalarGridSpec(
        num_scalar_prefetch=1,
        grid=(1, rows // tq, n_cache + n_new),
        in_specs=[
            pl.BlockSpec((1, tq, head_dim), q_map),
            pl.BlockSpec(
                (per_cache, prefix_dev, head_dim),
                lambda r, qi, ki, s: (c_block(ki, s), 0, 0),
            ),
            pl.BlockSpec(
                (per_cache, ext, prefix_dev),
                lambda r, qi, ki, s: (c_block(ki, s), 0, 0),
            ),
            pl.BlockSpec(
                (per_new, slot_dev, head_dim),
                lambda r, qi, ki, s: (n_block(qi, ki, s), new_at, 0),
            ),
            pl.BlockSpec(
                (per_new, ext, slot_dev),
                lambda r, qi, ki, s: (n_block(qi, ki, s), 0, new_at),
            ),
        ],
        out_specs=pl.BlockSpec((1, tq, head_dim), o_map),
        scratch_shapes=[
            pltpu.VMEM((1, tq), jnp.float32),
            pltpu.VMEM((ext, tq), jnp.float32),
        ],
    )
    return pl.pallas_call(
        kernel,
        grid_spec=grid_spec,
        out_shape=jax.ShapeDtypeStruct((1, rows, head_dim), jnp.bfloat16),
    )(scal, q, both, vt, both, vt)


def per_device(
    queries,
    new_kv,
    cache_kv,
    residual,
    prefix_len,
    dest_map,
    w_out,
    b_out,
    ln_gain,
    ln_bias,
    w_up,
    b_up,
    w_down,
    b_down,
):
    group = lax.axis_index("req")
    member = lax.axis_index("tok")
    n_group = lax.axis_size("req")
    n_member = lax.axis_size("tok")
    devices = n_group * n_member
    req_dev, slot_dev, width = queries.shape
    head_dim = new_kv.shape[2] // 2
    heads = width // head_dim
    own_prefix = lax.dynamic_slice_in_dim(prefix_len, group * req_dev, req_dev)
    live_count = jnp.sum((dest_map >= 0).astype(jnp.int32), axis=1)
    base = (member * slot_dev).astype(jnp.int32)
    rows = slot_dev * heads
    tq = min(2048, rows)
    tk = 1024
    q_flat = queries.reshape(req_dev, rows, head_dim)

    slots = req_dev * slot_dev
    capacity = (slots + devices - 1) // devices
    target = dest_map.reshape(slots)
    is_live = target >= 0
    peer = jnp.where(is_live, target // TOK_DEV, devices)
    onehot = (peer[:, None] == jnp.arange(devices, dtype=jnp.int32)[None, :]).astype(jnp.int32)
    position = jnp.sum((jnp.cumsum(onehot, axis=0) - 1) * onehot, axis=1)
    where_to = jnp.where(is_live, peer * capacity + position, devices * capacity)
    send_slots = devices * capacity
    pick = (
        where_to[None, :] == jnp.arange(send_slots, dtype=jnp.int32)[:, None]
    ).astype(jnp.bfloat16)
    row_ids = jnp.sum(
        jnp.where(
            where_to[None, :] == jnp.arange(send_slots, dtype=jnp.int32)[:, None],
            (target % TOK_DEV)[None, :] + 1,
            0,
        ),
        axis=1,
    ) - 1
    ids_in = lax.all_to_all(
        row_ids.reshape(devices, capacity),
        ("req", "tok"),
        split_axis=0,
        concat_axis=0,
        tiled=True,
    ).reshape(send_slots)
    prefix_dev = cache_kv.shape[1]
    local_kv = jnp.concatenate([cache_kv, new_kv], axis=1)
    if req_dev == 2:
        first = (own_prefix[1] > own_prefix[0]).astype(jnp.int32)
        order = [first, 1 - first]
    else:
        order = [jnp.int32(r) for r in range(req_dev)]
    gathered = [
        lax.all_gather(
            lax.dynamic_index_in_dim(local_kv, order[0], 0, keepdims=False),
            "tok",
            axis=0,
            tiled=True,
        )
    ]
    gathered[0], pick, ids_in = lax.optimization_barrier((gathered[0], pick, ids_in))
    for a in range(1, req_dev):
        mine = lax.dynamic_index_in_dim(local_kv, order[a], 0, keepdims=False)
        mine, gathered[-1] = lax.optimization_barrier((mine, gathered[-1]))
        gathered.append(lax.all_gather(mine, "tok", axis=0, tiled=True))
    outs = []
    for a in range(req_dev):
        r = order[a]
        both = gathered[a].reshape(n_member, prefix_dev + slot_dev, local_kv.shape[-1])
        own = lax.dynamic_index_in_dim(own_prefix, r, 0, keepdims=False)
        lives = lax.dynamic_index_in_dim(live_count, r, 0, keepdims=False)
        scal = jnp.stack([own, lives, base, r]).astype(jnp.int32)
        attended = flash_attention(
            q_flat, both, scal, heads, tq, tk, prefix_dev, slot_dev
        ).reshape(slot_dev, width)
        hidden_r = (
            lax.dynamic_index_in_dim(residual, r, 0, keepdims=False).astype(jnp.float32)
            + jnp.dot(attended, w_out, preferred_element_type=jnp.float32)
            + b_out
        ).astype(jnp.bfloat16)
        outs.append(
            jnp.dot(
                lax.dynamic_slice_in_dim(pick, r * slot_dev, slot_dev, axis=1),
                hidden_r,
                preferred_element_type=jnp.float32,
            )
        )
    send_rows = functools.reduce(jnp.add, outs).astype(jnp.bfloat16)
    rows_in = lax.all_to_all(
        send_rows.reshape(devices, capacity, width),
        ("req", "tok"),
        split_axis=0,
        concat_axis=0,
        tiled=True,
    ).reshape(send_slots, width)
    land = (ids_in[None, :] == jnp.arange(TOK_DEV, dtype=jnp.int32)[:, None]).astype(
        jnp.bfloat16
    )
    hidden_state = jnp.dot(land, rows_in, preferred_element_type=jnp.float32).astype(
        jnp.bfloat16
    )
    state_f = hidden_state.astype(jnp.float32)
    mean = jnp.mean(state_f, axis=-1, keepdims=True)
    centered = state_f - mean
    variance = jnp.mean(centered * centered, axis=-1, keepdims=True)
    normed = (centered * lax.rsqrt(variance + ln_eps) * ln_gain + ln_bias).astype(jnp.bfloat16)
    units = jax.nn.gelu(
        jnp.dot(
            lax.all_gather(normed, "tok", axis=0, tiled=True),
            w_up,
            preferred_element_type=jnp.float32,
        )
        + b_up,
        approximate=True,
    )
    terms = jnp.dot(units.astype(jnp.bfloat16), w_down, preferred_element_type=jnp.float32)
    summed = lax.psum_scatter(
        terms.astype(jnp.bfloat16), "tok", scatter_dimension=0, tiled=True
    ).astype(jnp.float32)
    return (state_f + summed + b_down).astype(jnp.bfloat16)


def solution(mesh):
    in_specs = (
        P("req", "tok", None),
        P("req", "tok", None),
        P("req", "tok", None),
        P("req", "tok", None),
        P(),
        P("req", "tok"),
        P(),
        P(),
        P(),
        P(),
        P(None, "tok"),
        P("tok"),
        P("tok", None),
        P(),
    )
    out_specs = P(("req", "tok"), None)
    return jax.shard_map(
        per_device, mesh=mesh, in_specs=in_specs, out_specs=out_specs, check_vma=False
    )
```

```python
import functools
import math

import jax
import jax.numpy as jnp
from jax import lax
from jax.experimental import pallas as pl
from jax.experimental.pallas import tpu as pltpu
from jax.sharding import PartitionSpec as P

TOK_DEV = 128


neg_large = -1e30
ln_eps = 1e-05


def flash_kernel(
    scal_ref,
    q_ref,
    ck_ref,
    cv_ref,
    nk_ref,
    nv_ref,
    o_ref,
    m_sc,
    acc_sc,
    *,
    tq,
    tk,
    heads,
    head_dim,
    n_cache,
    scale,
):
    qi = pl.program_id(1)
    ki = pl.program_id(2)
    prefix = scal_ref[0]
    live = scal_ref[1]
    base = scal_ref[2]
    spt = tq // heads
    tile_lo = qi * spt
    tile_live = tile_lo < live
    q_lo = base + tile_lo
    q_hi = q_lo + spt - 1

    @pl.when(ki == 0)
    def _init():
        m_sc[...] = jnp.full(m_sc.shape, neg_large, jnp.float32)
        acc_sc[...] = jnp.zeros(acc_sc.shape, jnp.float32)

    def step(k_ref, v_ref, mask_fn):
        pieces, chunk = k_ref.shape[0], k_ref.shape[1]
        k = k_ref[...].reshape(pieces * chunk, head_dim)
        s = (
            lax.dot_general(
                k, q_ref[0], (((1,), (1,)), ((), ())), preferred_element_type=jnp.float32
            )
            * scale
        )
        mask = None
        if mask_fn is not None:
            mask = mask_fn()
            s = jnp.where(mask, s, neg_large)
        m_prev = m_sc[...]
        m_new = jnp.maximum(m_prev, jnp.max(s, axis=0, keepdims=True))
        p = jnp.exp(s - m_new)
        if mask is not None:
            p = jnp.where(mask, p, 0.0)
        alpha = jnp.exp(m_prev - m_new)
        pb = p.astype(jnp.bfloat16)
        total = alpha * acc_sc[...]
        for piece in range(pieces):
            total = total + jnp.dot(
                v_ref[piece],
                pb[piece * chunk : (piece + 1) * chunk],
                preferred_element_type=jnp.float32,
            )
        acc_sc[...] = total
        m_sc[...] = m_new

    is_cache = ki < n_cache
    kc = ki * tk
    kn = (ki - n_cache) * tk
    run_cache = is_cache & tile_live & (kc < prefix)
    full_cache = kc + tk <= prefix
    run_new = jnp.logical_not(is_cache) & tile_live & (kn <= q_hi)
    full_new = kn + tk - 1 <= q_lo

    def cache_mask():
        key = lax.broadcasted_iota(jnp.int32, (tk, tq), 0) + kc
        return key < prefix

    def new_mask():
        key = lax.broadcasted_iota(jnp.int32, (tk, tq), 0) + kn
        slot = lax.broadcasted_iota(jnp.int32, (tk, tq), 1) // heads + q_lo
        return key <= slot

    @pl.when(run_cache & full_cache)
    def _c_full():
        step(ck_ref, cv_ref, None)

    @pl.when(run_cache & jnp.logical_not(full_cache))
    def _c_part():
        step(ck_ref, cv_ref, cache_mask)

    @pl.when(run_new & full_new)
    def _n_full():
        step(nk_ref, nv_ref, None)

    @pl.when(run_new & jnp.logical_not(full_new))
    def _n_part():
        step(nk_ref, nv_ref, new_mask)

    @pl.when(ki == pl.num_programs(2) - 1)
    def _fin():
        acc = acc_sc[...]
        l = acc[head_dim : head_dim + 1]
        safe = jnp.where(l > 0, l, 1.0)
        out = jnp.where(l > 0, acc[:head_dim] / safe, 0.0)
        o_ref[0] = jnp.transpose(out).astype(o_ref.dtype)


def flash_attention(q, req, both, scal, heads, tq, tk, prefix_dev, slot_dev):
    n_req, rows, head_dim = q.shape
    n_member = both.shape[0]
    n_cache = n_member * prefix_dev // tk
    n_new = n_member * slot_dev // tk
    per_cache = tk // prefix_dev
    per_new = tk // slot_dev
    new_at = prefix_dev // slot_dev
    spt = tq // heads
    scale = 1.0 / math.sqrt(head_dim)
    ones = jnp.ones((n_member, 8, both.shape[1]), jnp.bfloat16)
    vt = jnp.concatenate([jnp.swapaxes(both[:, :, head_dim:], 1, 2), ones], axis=1)
    ext = head_dim + 8

    def q_map(r, qi, ki, s):
        return (req, qi, 0)

    def o_map(r, qi, ki, s):
        return (0, qi, 0)

    def c_block(ki, s):
        last = jnp.maximum((s[0] + tk - 1) // tk - 1, 0)
        return jnp.minimum(ki, last)

    def n_block(qi, ki, s):
        q_hi = s[2] + (qi + 1) * spt - 1
        last = jnp.minimum(q_hi // tk, n_new - 1)
        return jnp.clip(ki - n_cache, 0, last)

    kernel = functools.partial(
        flash_kernel,
        tq=tq,
        tk=tk,
        heads=heads,
        head_dim=head_dim,
        n_cache=n_cache,
        scale=scale,
    )
    grid_spec = pltpu.PrefetchScalarGridSpec(
        num_scalar_prefetch=1,
        grid=(1, rows // tq, n_cache + n_new),
        in_specs=[
            pl.BlockSpec((1, tq, head_dim), q_map),
            pl.BlockSpec(
                (per_cache, prefix_dev, head_dim),
                lambda r, qi, ki, s: (c_block(ki, s), 0, 0),
            ),
            pl.BlockSpec(
                (per_cache, ext, prefix_dev),
                lambda r, qi, ki, s: (c_block(ki, s), 0, 0),
            ),
            pl.BlockSpec(
                (per_new, slot_dev, head_dim),
                lambda r, qi, ki, s: (n_block(qi, ki, s), new_at, 0),
            ),
            pl.BlockSpec(
                (per_new, ext, slot_dev),
                lambda r, qi, ki, s: (n_block(qi, ki, s), 0, new_at),
            ),
        ],
        out_specs=pl.BlockSpec((1, tq, head_dim), o_map),
        scratch_shapes=[
            pltpu.VMEM((1, tq), jnp.float32),
            pltpu.VMEM((ext, tq), jnp.float32),
        ],
    )
    return pl.pallas_call(
        kernel,
        grid_spec=grid_spec,
        out_shape=jax.ShapeDtypeStruct((1, rows, head_dim), jnp.bfloat16),
    )(scal, q, both, vt, both, vt)


def per_device(
    queries,
    new_kv,
    cache_kv,
    residual,
    prefix_len,
    dest_map,
    w_out,
    b_out,
    ln_gain,
    ln_bias,
    w_up,
    b_up,
    w_down,
    b_down,
):
    group = lax.axis_index("req")
    member = lax.axis_index("tok")
    n_group = lax.axis_size("req")
    n_member = lax.axis_size("tok")
    devices = n_group * n_member
    req_dev, slot_dev, width = queries.shape
    head_dim = new_kv.shape[2] // 2
    heads = width // head_dim
    own_prefix = lax.dynamic_slice_in_dim(prefix_len, group * req_dev, req_dev)
    live_count = jnp.sum((dest_map >= 0).astype(jnp.int32), axis=1)
    base = (member * slot_dev).astype(jnp.int32)
    rows = slot_dev * heads
    tq = min(2048, rows)
    tk = 1024
    q_flat = queries.reshape(req_dev, rows, head_dim)

    slots = req_dev * slot_dev
    capacity = (slots + devices - 1) // devices
    target = dest_map.reshape(slots)
    is_live = target >= 0
    peer = jnp.where(is_live, target // TOK_DEV, devices)
    onehot = (peer[:, None] == jnp.arange(devices, dtype=jnp.int32)[None, :]).astype(jnp.int32)
    position = jnp.sum((jnp.cumsum(onehot, axis=0) - 1) * onehot, axis=1)
    where_to = jnp.where(is_live, peer * capacity + position, devices * capacity)
    send_slots = devices * capacity
    pick = (
        where_to[None, :] == jnp.arange(send_slots, dtype=jnp.int32)[:, None]
    ).astype(jnp.bfloat16)
    row_ids = jnp.sum(
        jnp.where(
            where_to[None, :] == jnp.arange(send_slots, dtype=jnp.int32)[:, None],
            (target % TOK_DEV)[None, :] + 1,
            0,
        ),
        axis=1,
    ) - 1
    ids_in = lax.all_to_all(
        row_ids.reshape(devices, capacity),
        ("req", "tok"),
        split_axis=0,
        concat_axis=0,
        tiled=True,
    ).reshape(send_slots)
    prefix_dev = cache_kv.shape[1]
    local_kv = jnp.concatenate([cache_kv, new_kv], axis=1)
    gathered = [lax.all_gather(local_kv[0], "tok", axis=0, tiled=True)]
    scals = [
        jnp.stack([own_prefix[r], live_count[r], base]).astype(jnp.int32)
        for r in range(req_dev)
    ]
    gathered[0], pick, ids_in, q_flat, scals = lax.optimization_barrier(
        (gathered[0], pick, ids_in, q_flat, scals)
    )
    for r in range(1, req_dev):
        mine, gathered[-1] = lax.optimization_barrier((local_kv[r], gathered[-1]))
        gathered.append(lax.all_gather(mine, "tok", axis=0, tiled=True))
    outs = []
    for r in range(req_dev):
        both = gathered[r].reshape(n_member, prefix_dev + slot_dev, local_kv.shape[-1])
        scal = scals[r]
        attended = flash_attention(
            q_flat, r, both, scal, heads, tq, tk, prefix_dev, slot_dev
        ).reshape(slot_dev, width)
        hidden_r = (
            residual[r].astype(jnp.float32)
            + jnp.dot(attended, w_out, preferred_element_type=jnp.float32)
            + b_out
        ).astype(jnp.bfloat16)
        outs.append(
            jnp.dot(
                pick[:, r * slot_dev : (r + 1) * slot_dev],
                hidden_r,
                preferred_element_type=jnp.float32,
            )
        )
    send_rows = functools.reduce(jnp.add, outs).astype(jnp.bfloat16)
    rows_in = lax.all_to_all(
        send_rows.reshape(devices, capacity, width),
        ("req", "tok"),
        split_axis=0,
        concat_axis=0,
        tiled=True,
    ).reshape(send_slots, width)
    land = (ids_in[None, :] == jnp.arange(TOK_DEV, dtype=jnp.int32)[:, None]).astype(
        jnp.bfloat16
    )
    hidden_state = jnp.dot(land, rows_in, preferred_element_type=jnp.float32).astype(
        jnp.bfloat16
    )
    state_f = hidden_state.astype(jnp.float32)
    mean = jnp.mean(state_f, axis=-1, keepdims=True)
    centered = state_f - mean
    variance = jnp.mean(centered * centered, axis=-1, keepdims=True)
    normed = (centered * lax.rsqrt(variance + ln_eps) * ln_gain + ln_bias).astype(jnp.bfloat16)
    units = jax.nn.gelu(
        jnp.dot(
            lax.all_gather(normed, "tok", axis=0, tiled=True),
            w_up,
            preferred_element_type=jnp.float32,
        )
        + b_up,
        approximate=True,
    )
    terms = jnp.dot(units.astype(jnp.bfloat16), w_down, preferred_element_type=jnp.float32)
    summed = lax.psum_scatter(
        terms.astype(jnp.bfloat16), "tok", scatter_dimension=0, tiled=True
    ).astype(jnp.float32)
    return (state_f + summed + b_down).astype(jnp.bfloat16)


def solution(mesh):
    in_specs = (
        P("req", "tok", None),
        P("req", "tok", None),
        P("req", "tok", None),
        P("req", "tok", None),
        P(),
        P("req", "tok"),
        P(),
        P(),
        P(),
        P(),
        P(None, "tok"),
        P("tok"),
        P("tok", None),
        P(),
    )
    out_specs = P(("req", "tok"), None)
    return jax.shard_map(
        per_device, mesh=mesh, in_specs=in_specs, out_specs=out_specs, check_vma=False
    )
```
